256 devices in a mesh: rect: 64 (over z, x, core), split: 4 (over y).
Axes of the slice: x: 4, y: 4, z: 8, core: 2. Of those that a mesh axis runs over, the one named last changes fastest.
Arguments:
- small_now: float32 [512, 16, 16, 384], P(('rect', 'split')), may hold values from -6 to 6
- small_prev: float32 [512, 16, 16, 384], P(('rect', 'split')), may hold values from -6 to 6
- plaza_now: float32 [64, 64, 16, 384], P('rect', 'split'), may hold values from -6 to 6
- plaza_prev: float32 [64, 64, 16, 384], P('rect', 'split'), may hold values from -6 to 6
- face_partner: int32 [64, 4, 96], P('rect', 'split'), may hold values from -1 to 6143, as said below
Outputs:
- small_modes: float32 [512, 16, 16, 384], P(('rect', 'split'))
- small_before: float32 [512, 16, 16, 384], P(('rect', 'split'))
- plaza_modes: float32 [64, 64, 16, 384], P('rect', 'split')
- plaza_before: float32 [64, 64, 16, 384], P('rect', 'split')
The draws below stay inside these ranges and needn't reach their ends.
Inputs may be any that keep to these rules, and one draw needn't show every extreme that they name: `face_partner`: an entry of group (r, s) is -1 or r2 * 96 + e2, segment e2 of group (r2, s) with the same s and r2 != r, of the same piece number. Pairing is symmetric; side 1 pairs with side 0 and side 3 with side 2. Every segment is paired except those of sides 0 and 1 of block 2, which are -1. At most 2 segments of one group pair with segments of any one group, and exactly 2 in some pair of groups.
All inputs are finite; a program needn't handle non-finite values.
Results may differ from the reference program's by a relative error of at most 0.0001.
Values sent between devices are 32-bit elements; how exact they have to be, the bound alone decides.
No kernel may reach another device: no remote copies, remote signals or barrier semaphores. Data moves between devices by JAX's collectives and lax.ppermute only.
A program may use at most 64 MiB of HBM per device.

```python
import jax
import jax.numpy as jnp
from jax import lax

SIDE = 16
HEIGHT = 384
R_DEV = 2
STEPS = 2
PIECES = 8
SEG = 2
MOST = 2
SLABS = 4
PLAZAS = 64
PX = 64
FACES_DEV = 12
SEGS_DEV = 96
RECTS = 512


def column_table(column_key):
    blocks = R_DEV + 1
    pair_kinds = 2 * R_DEV + 1
    unit_count = pair_kinds * PIECES
    offset_count = PLAZAS // 2 - 1
    subkeys = jax.random.split(column_key, 7)
    relabel = jax.random.permutation(subkeys[0], PLAZAS).astype(jnp.int32)
    restore = jnp.zeros((PLAZAS,), jnp.int32).at[relabel].set(jnp.arange(PLAZAS, dtype=jnp.int32))
    offsets = (jax.random.permutation(subkeys[1], offset_count) + 1).astype(jnp.int32)
    unit_shift = offsets[jnp.arange(unit_count) // MOST]
    unit_shift = unit_shift[jax.random.permutation(subkeys[2], unit_count)]
    high_x_order = jax.vmap(lambda sub: jax.random.permutation(sub, R_DEV))(jax.random.split(subkeys[3], PLAZAS)).astype(jnp.int32)
    low_x_order = jax.vmap(lambda sub: jax.random.permutation(sub, R_DEV))(jax.random.split(subkeys[4], PLAZAS)).astype(jnp.int32)
    high_y_order = jax.vmap(lambda sub: jax.random.permutation(sub, blocks))(jax.random.split(subkeys[5], PLAZAS)).astype(jnp.int32)
    low_y_order = jax.vmap(lambda sub: jax.random.permutation(sub, blocks))(jax.random.split(subkeys[6], PLAZAS)).astype(jnp.int32)
    partner_table = jnp.full((PLAZAS, blocks, 4, PIECES), -1, jnp.int32)
    group_rows = jnp.arange(PLAZAS, dtype=jnp.int32)
    for pair_kind in range(pair_kinds):
        if pair_kind < R_DEV:
            high_order, low_order, column_index, high_side, low_side = (high_x_order, low_x_order, pair_kind, 1, 0)
        else:
            high_order, low_order, column_index, high_side, low_side = (high_y_order, low_y_order, pair_kind - R_DEV, 3, 2)
        high_block = high_order[:, column_index]
        low_block = low_order[:, column_index]
        for piece in range(PIECES):
            shift = unit_shift[pair_kind * PIECES + piece]
            forward = restore[(relabel + shift) % PLAZAS]
            backward = restore[(relabel - shift) % PLAZAS]
            partner_table = partner_table.at[group_rows, high_block, high_side, piece].set(forward * SEGS_DEV + (low_order[forward, column_index] * 4 + low_side) * PIECES + piece)
            partner_table = partner_table.at[group_rows, low_block, low_side, piece].set(backward * SEGS_DEV + (high_order[backward, column_index] * 4 + high_side) * PIECES + piece)
    return partner_table.reshape(PLAZAS, blocks * 4 * PIECES)


def draw_face_partner(key, part):
    tables = jax.vmap(column_table)(jax.random.split(key, SLABS))
    return jnp.transpose(tables, (1, 0, 2)).astype(jnp.int32)


def block_levels(rng, shape, pieces, smallest, top_value):
    def one(dim, blocks):
        steps = jax.random.uniform(jax.random.fold_in(jax.random.fold_in(rng, 6), dim), (blocks,), jnp.float32, smallest / len(pieces), top_value / len(pieces))
        return jnp.repeat(jnp.exp(steps), shape[dim] // blocks).reshape((-1,) + (1,) * (len(shape) - dim - 1))

    gain = one(*pieces[0])
    for cut in pieces[1:]:
        gain = gain * one(*cut)
    return gain


def gaussian(stream_key, dims, width, reach, cuts=(), held_as=jnp.bfloat16):
    entries = width * jax.random.normal(stream_key, dims, jnp.float32)
    if cuts:
        entries = entries * block_levels(stream_key, dims, cuts, -0.22, 0.18)
    return jnp.clip(entries, -reach, reach).astype(held_as)


def setup_inputs(seed: int = 0) -> dict:
    key_list = jax.random.split(jax.random.key(seed), 6)
    return {
        "small_now": gaussian(key_list[0], (RECTS, SIDE, SIDE, HEIGHT), 1.0, 6.0, ((0, 256),), jnp.float32),
        "small_prev": gaussian(key_list[1], (RECTS, SIDE, SIDE, HEIGHT), 1.0, 6.0, ((0, 256),), jnp.float32),
        "plaza_now": gaussian(key_list[2], (PLAZAS, PX, SIDE, HEIGHT), 1.0, 6.0, ((0, 64), (1, 4)), jnp.float32),
        "plaza_prev": gaussian(key_list[3], (PLAZAS, PX, SIDE, HEIGHT), 1.0, 6.0, ((0, 64), (1, 4)), jnp.float32),
        "face_partner": draw_face_partner(jax.random.fold_in(key_list[5], 71), 0),
    }


COURANT = 0.5
highest = lax.Precision.HIGHEST

def dct_table(length):
    wavenumber = jnp.arange(length, dtype=jnp.float32)[:, None]
    position = jnp.arange(length, dtype=jnp.float32)[None, :]
    weight = jnp.where(wavenumber == 0.0, jnp.sqrt(1.0 / length), jnp.sqrt(2.0 / length))
    return (weight * jnp.cos(jnp.pi * wavenumber * (position + 0.5) / length)).astype(jnp.float32)

def along_z(values, matrix):
    return jnp.einsum('...k,kz->...z', values, matrix, precision=highest)

def along_y(values, matrix):
    return jnp.einsum('...kz,ky->...yz', values, matrix, precision=highest)

def along_x(values, matrix):
    return jnp.einsum('...kyz,kx->...xyz', values, matrix, precision=highest)

def inverse_three(spectrum, matrix_x, matrix_y, matrix_z):
    return along_x(along_y(along_z(spectrum, matrix_z), matrix_y), matrix_x)

def forward_three(values, matrix_x, matrix_y, matrix_z):
    return along_x(along_y(along_z(values, matrix_z.T), matrix_y.T), matrix_x.T)

def update_factors(first_row, row_count, length_x, edge_cells, height_cells):
    wave_x = (first_row + jnp.arange(row_count)).astype(jnp.float32)[:, None, None] / length_x
    wave_y = jnp.arange(edge_cells, dtype=jnp.float32)[None, :, None] / edge_cells
    wave_z = jnp.arange(height_cells, dtype=jnp.float32)[None, None, :] / height_cells
    phase_angle = COURANT * jnp.pi * jnp.sqrt(wave_x ** 2 + wave_y ** 2 + wave_z ** 2)
    twice_cos = 2.0 * jnp.cos(phase_angle)
    forcing_gain = COURANT ** 2 * jnp.sinc(phase_angle / (2.0 * jnp.pi)) ** 2
    return (twice_cos, forcing_gain)

def face_strips(pressure):
    low_x = pressure[..., 0:3, :, :]
    high_x = jnp.flip(pressure[..., -3:, :, :], axis=-3)
    low_y = jnp.swapaxes(pressure[..., :, 0:3, :], -3, -2)
    high_y = jnp.swapaxes(jnp.flip(pressure[..., :, -3:, :], axis=-2), -3, -2)
    return jnp.stack([low_x, high_x, low_y, high_y], axis=-4)

def interface_layers(difference):
    nearest = difference[..., 0, :, :]
    middle = difference[..., 1, :, :]
    farthest = difference[..., 2, :, :]
    return jnp.stack([(270.0 * nearest - 27.0 * middle + 2.0 * farthest) / 180.0, (-27.0 * nearest + 2.0 * middle) / 180.0, 2.0 * nearest / 180.0], axis=-3)

def forcing_volume(layers):
    edge_cells = layers.shape[-2]
    padding = jnp.zeros(layers.shape[:-4] + (edge_cells - 3, edge_cells, layers.shape[-1]), layers.dtype)

    def widened(layer_set):
        return jnp.concatenate([layer_set, padding], axis=-3)
    low_x = widened(layers[..., 0, :, :, :])
    high_x = jnp.flip(widened(layers[..., 1, :, :, :]), axis=-3)
    low_y = jnp.swapaxes(widened(layers[..., 2, :, :, :]), -3, -2)
    high_y = jnp.swapaxes(jnp.flip(widened(layers[..., 3, :, :, :]), axis=-3), -3, -2)
    return low_x + high_x + low_y + high_y

def reference(small_now, small_prev, plaza_now, plaza_prev, face_partner):
    table_side = dct_table(SIDE)
    table_height = dct_table(HEIGHT)
    table_plaza = dct_table(PX)
    small_cos, small_gain = update_factors(0, SIDE, SIDE, SIDE, HEIGHT)
    plaza_cos, plaza_gain = update_factors(0, PX, PX, SIDE, HEIGHT)
    paired = face_partner >= 0
    partner_id = jnp.where(paired, face_partner, 0)
    other_group = partner_id // SEGS_DEV
    other_seg = partner_id % SEGS_DEV
    column = jnp.broadcast_to(jnp.arange(SLABS, dtype=jnp.int32)[None, :, None], face_partner.shape)
    for time_step in range(STEPS):
        small_field = inverse_three(small_now, table_side, table_side, table_height)
        plaza_field = inverse_three(plaza_now, table_plaza, table_side, table_height)
        blocks = jnp.concatenate([small_field.reshape(PLAZAS, SLABS, R_DEV, SIDE, SIDE, HEIGHT), plaza_field.reshape(PLAZAS, SLABS, 1, SIDE, SIDE, HEIGHT)], axis=2)
        strips = face_strips(blocks).reshape(PLAZAS, SLABS, FACES_DEV, 3, PIECES, SEG, HEIGHT)
        segments = jnp.transpose(strips, (0, 1, 2, 4, 3, 5, 6)).reshape(PLAZAS, SLABS, SEGS_DEV, 3, SEG, HEIGHT)
        remote = segments[other_group, column, other_seg]
        difference = jnp.where(paired[..., None, None, None], remote - segments, 0.0)
        difference = difference.reshape(PLAZAS, SLABS, FACES_DEV, PIECES, 3, SEG, HEIGHT)
        difference = jnp.transpose(difference, (0, 1, 2, 4, 3, 5, 6)).reshape(PLAZAS, SLABS, FACES_DEV, 3, SIDE, HEIGHT)
        layers = interface_layers(difference).reshape(PLAZAS, SLABS, R_DEV + 1, 4, 3, SIDE, HEIGHT)
        volume = forcing_volume(layers)
        small_force = forward_three(volume[:, :, :R_DEV].reshape(RECTS, SIDE, SIDE, HEIGHT), table_side, table_side, table_height)
        plaza_force = forward_three(volume[:, :, R_DEV].reshape(PLAZAS, PX, SIDE, HEIGHT), table_plaza, table_side, table_height)
        small_next = small_cos * small_now - small_prev + small_gain * small_force
        plaza_next = plaza_cos * plaza_now - plaza_prev + plaza_gain * plaza_force
        small_prev, small_now = (small_now, small_next)
        plaza_prev, plaza_now = (plaza_now, plaza_next)
    return (small_now, small_prev, plaza_now, plaza_prev)
```

```python
import jax
import jax.numpy as jnp
from jax import lax
from jax.sharding import PartitionSpec as P

STEPS = 2
COURANT = 0.5
highest = lax.Precision.HIGHEST


def dct_rows_cols(wavenumber, position, length):
    wavenumber = wavenumber.astype(jnp.float32)[:, None]
    position = position.astype(jnp.float32)[None, :]
    weight = jnp.where(wavenumber == 0.0, jnp.sqrt(1.0 / length), jnp.sqrt(2.0 / length))
    return weight * jnp.cos(jnp.pi * wavenumber * (position + 0.5) / length)


def dct_table(length):
    return dct_rows_cols(jnp.arange(length), jnp.arange(length), length)


def update_factors(first_row, row_count, length_x, edge_cells, height_cells):
    wave_x = (first_row + jnp.arange(row_count)).astype(jnp.float32)[:, None, None] / length_x
    wave_y = jnp.arange(edge_cells, dtype=jnp.float32)[None, :, None] / edge_cells
    wave_z = jnp.arange(height_cells, dtype=jnp.float32)[None, None, :] / height_cells
    phase_angle = COURANT * jnp.pi * jnp.sqrt(wave_x**2 + wave_y**2 + wave_z**2)
    twice_cos = 2.0 * jnp.cos(phase_angle)
    forcing_gain = COURANT**2 * jnp.sinc(phase_angle / (2.0 * jnp.pi)) ** 2
    return (twice_cos, forcing_gain)


def interface_layers(difference):
    nearest = difference[:, 0]
    middle = difference[:, 1]
    farthest = difference[:, 2]
    return jnp.stack(
        [
            (270.0 * nearest - 27.0 * middle + 2.0 * farthest) / 180.0,
            (-27.0 * nearest + 2.0 * middle) / 180.0,
            2.0 * nearest / 180.0,
        ],
        axis=1,
    )


def ein(spec, a, b):
    return jnp.einsum(spec, a, b, precision=highest, preferred_element_type=jnp.float32)


def on_device(small_now, small_prev, plaza_now, plaza_prev, face_partner):
    owned = small_now.shape[0]
    edge = small_now.shape[1]
    height = small_now.shape[3]
    slabs = lax.axis_size("split")
    groups = lax.axis_size("rect")
    plaza_len = edge * slabs
    first_row = lax.axis_index("split") * edge

    table_side = dct_table(edge)
    table_height = dct_table(height)
    edge_pos = jnp.array([0, 1, 2, edge - 1, edge - 2, edge - 3], jnp.int32)
    side6 = table_side[:, edge_pos]
    mine = first_row + jnp.arange(edge)
    plaza_cols = dct_rows_cols(jnp.arange(plaza_len), mine, plaza_len)
    plaza_rows = dct_rows_cols(mine, jnp.arange(plaza_len), plaza_len)

    small_cos, small_gain = update_factors(0, edge, edge, edge, height)
    plaza_cos, plaza_gain = update_factors(first_row, edge, plaza_len, edge, height)

    partners = face_partner.reshape(-1)
    seg_count = partners.shape[0]
    face_count = 4 * (owned + 1)
    pieces = seg_count // face_count
    seg_cells = edge // pieces
    unit_count = (2 * owned + 1) * pieces
    slot_most = (unit_count + groups // 2 - 2) // (groups // 2 - 1)
    slots = groups * slot_most
    paired = partners >= 0
    partner_id = jnp.where(paired, partners, 0)
    other_group = partner_id // seg_count
    other_seg = partner_id % seg_count
    same_group = (other_group[:, None] == other_group[None, :]) & paired[:, None] & paired[None, :]
    send_rank = jnp.sum(same_group & (other_seg[None, :] < other_seg[:, None]), axis=1)
    seg_order = jnp.arange(seg_count)
    recv_rank = jnp.sum(same_group & (seg_order[None, :] < seg_order[:, None]), axis=1)
    target = jnp.where(paired, other_group * slot_most + send_rank, -1)
    source = jnp.where(paired, other_group * slot_most + recv_rank, -1)
    slot_ids = jnp.arange(slots)
    send_hot = (slot_ids[:, None] == target[None, :]).astype(jnp.float32)
    send_hot = send_hot.reshape(slots, face_count, pieces)
    recv_hot = (source[:, None] == slot_ids[None, :]).astype(jnp.float32)
    recv_hot = recv_hot.reshape(face_count, pieces, slots)
    pair_mask = paired.reshape(face_count, 1, pieces, 1, 1)

    small_old, small_cur = small_prev, small_now
    plaza_old, plaza_cur = plaza_prev[0], plaza_now[0]
    for _ in range(STEPS):
        along_z = ein("bijk,zk->bijz", small_cur, table_height.T)
        x_faces = ein("bxjz,jy->bxyz", ein("bijz,ix->bxjz", along_z, side6), table_side)
        y_faces = ein("byiz,ix->byxz", ein("bijz,jy->byiz", along_z, side6), table_side)
        small_strips = jnp.concatenate([x_faces, y_faces], axis=1)
        small_strips = small_strips.reshape(owned * 4, 3, edge, height)
        plaza_z = ein("ijk,zk->ijz", plaza_cur, table_height.T)
        plaza_y = ein("ijz,jy->yiz", plaza_z, side6)
        plaza_all = lax.all_gather(plaza_y, "split", axis=1, tiled=True)
        plaza_faces = ein("yiz,ix->yxz", plaza_all, plaza_cols)
        plaza_strips = jnp.concatenate(
            [jnp.zeros_like(plaza_faces), plaza_faces], axis=0
        ).reshape(4, 3, edge, height)
        strips = jnp.concatenate([small_strips, plaza_strips], axis=0)
        segments = strips.reshape(face_count, 3, pieces, seg_cells, height)
        outgoing = ein("sfq,fmqcz->smcz", send_hot, segments)
        arrived = lax.all_to_all(outgoing, "rect", 0, 0, tiled=True)
        remote = ein("fqs,smcz->fmqcz", recv_hot, arrived)
        difference = jnp.where(pair_mask, remote - segments, 0.0)
        layers = interface_layers(difference.reshape(face_count, 3, edge, height))
        layers_z = ein("fmuz,kz->fmuk", layers, table_height)
        small_layers = layers_z[: owned * 4].reshape(owned, 12, edge, height)
        small_force = ein(
            "biyk,jy->bijk", ein("bxyk,ix->biyk", small_layers[:, :6], side6), table_side
        ) + ein("bjxk,ix->bijk", ein("byxk,jy->bjxk", small_layers[:, 6:], side6), table_side)
        plaza_layers = layers_z[owned * 4 + 2 :].reshape(6, edge, height)
        plaza_gathered = lax.all_gather(plaza_layers, "split", axis=1, tiled=True)
        plaza_x = ein("yxk,ix->yik", plaza_gathered, plaza_rows)
        plaza_force = ein("yik,jy->ijk", plaza_x, side6)
        small_next = small_cos * small_cur - small_old + small_gain * small_force
        plaza_next = plaza_cos * plaza_cur - plaza_old + plaza_gain * plaza_force
        small_old, small_cur = small_cur, small_next
        plaza_old, plaza_cur = plaza_cur, plaza_next
    return (small_cur, small_old, plaza_cur[None], plaza_old[None])


def solution(mesh):
    return jax.shard_map(
        on_device,
        mesh=mesh,
        in_specs=(
            P(("rect", "split"), None, None, None),
            P(("rect", "split"), None, None, None),
            P("rect", "split", None, None),
            P("rect", "split", None, None),
            P("rect", "split", None),
        ),
        out_specs=(
            P(("rect", "split"), None, None, None),
            P(("rect", "split"), None, None, None),
            P("rect", "split", None, None),
            P("rect", "split", None, None),
        ),
        check_vma=False,
    )
```

```python
import jax
import jax.numpy as jnp
from jax import lax
from jax.sharding import PartitionSpec as P

STEPS = 2
COURANT = 0.5
highest = lax.Precision.HIGHEST


def dct_rows_cols(wavenumber, position, length):
    wavenumber = wavenumber.astype(jnp.float32)[:, None]
    position = position.astype(jnp.float32)[None, :]
    weight = jnp.where(wavenumber == 0.0, jnp.sqrt(1.0 / length), jnp.sqrt(2.0 / length))
    return weight * jnp.cos(jnp.pi * wavenumber * (position + 0.5) / length)


def dct_table(length):
    return dct_rows_cols(jnp.arange(length), jnp.arange(length), length)


def update_factors(first_row, row_count, length_x, edge_cells, height_cells):
    wave_x = (first_row + jnp.arange(row_count)).astype(jnp.float32)[:, None, None] / length_x
    wave_y = jnp.arange(edge_cells, dtype=jnp.float32)[None, :, None] / edge_cells
    wave_z = jnp.arange(height_cells, dtype=jnp.float32)[None, None, :] / height_cells
    phase_angle = COURANT * jnp.pi * jnp.sqrt(wave_x**2 + wave_y**2 + wave_z**2)
    twice_cos = 2.0 * jnp.cos(phase_angle)
    forcing_gain = COURANT**2 * jnp.sinc(phase_angle / (2.0 * jnp.pi)) ** 2
    return (twice_cos, forcing_gain)


def interface_layers(difference):
    nearest = difference[:, 0]
    middle = difference[:, 1]
    farthest = difference[:, 2]
    return jnp.stack(
        [
            (270.0 * nearest - 27.0 * middle + 2.0 * farthest) / 180.0,
            (-27.0 * nearest + 2.0 * middle) / 180.0,
            2.0 * nearest / 180.0,
        ],
        axis=1,
    )


def ein(spec, a, b):
    return jnp.einsum(spec, a, b, precision=highest, preferred_element_type=jnp.float32)


def on_device(small_now, small_prev, plaza_now, plaza_prev, face_partner):
    owned = small_now.shape[0]
    edge = small_now.shape[1]
    height = small_now.shape[3]
    slabs = lax.axis_size("split")
    groups = lax.axis_size("rect")
    plaza_len = edge * slabs
    first_row = lax.axis_index("split") * edge

    table_side = dct_table(edge)
    table_height = dct_table(height)
    edge_pos = jnp.array([0, 1, 2, edge - 1, edge - 2, edge - 3], jnp.int32)
    side6 = table_side[:, edge_pos]
    mine = first_row + jnp.arange(edge)
    plaza_cols = dct_rows_cols(jnp.arange(plaza_len), mine, plaza_len)
    plaza_rows = dct_rows_cols(mine, jnp.arange(plaza_len), plaza_len)

    small_cos, small_gain = update_factors(0, edge, edge, edge, height)
    plaza_cos, plaza_gain = update_factors(first_row, edge, plaza_len, edge, height)

    partners = face_partner.reshape(-1)
    seg_count = partners.shape[0]
    face_count = 4 * (owned + 1)
    pieces = seg_count // face_count
    seg_cells = edge // pieces
    unit_count = (2 * owned + 1) * pieces
    slot_most = (unit_count + groups // 2 - 2) // (groups // 2 - 1)
    slots = groups * slot_most
    paired = partners >= 0
    partner_id = jnp.where(paired, partners, 0)
    other_group = partner_id // seg_count
    other_seg = partner_id % seg_count
    same_group = (other_group[:, None] == other_group[None, :]) & paired[:, None] & paired[None, :]
    send_rank = jnp.sum(same_group & (other_seg[None, :] < other_seg[:, None]), axis=1)
    seg_order = jnp.arange(seg_count)
    recv_rank = jnp.sum(same_group & (seg_order[None, :] < seg_order[:, None]), axis=1)
    target = jnp.where(paired, other_group * slot_most + send_rank, -1)
    source = jnp.where(paired, other_group * slot_most + recv_rank, -1)
    slot_ids = jnp.arange(slots)
    send_hot = (slot_ids[:, None] == target[None, :]).astype(jnp.float32)
    send_hot = send_hot.reshape(slots, face_count, pieces)
    recv_hot = (source[:, None] == slot_ids[None, :]).astype(jnp.float32)
    recv_hot = recv_hot.reshape(face_count, pieces, slots)
    pair_mask = paired.reshape(face_count, 1, pieces, 1, 1)

    x_rows = side6[:, None, :, None] * table_side[None, :, None, :]
    y_rows = table_side[:, None, None, :] * side6[None, :, :, None]
    face_rows = jnp.concatenate(
        [x_rows.reshape(edge * edge, 6 * edge), y_rows.reshape(edge * edge, 6 * edge)], axis=1
    )

    small_old, small_cur = small_prev, small_now
    plaza_old, plaza_cur = plaza_prev[0], plaza_now[0]
    for _ in range(STEPS):
        flat_modes = small_cur.reshape(owned, edge * edge, height)
        small_strips = ein("rz,zk->rk", ein("pr,bpk->brk", face_rows, flat_modes).reshape(-1, height), table_height)
        small_strips = small_strips.reshape(owned * 4, 3, edge, height)
        plaza_y = ein("iyk,kz->iyz", ein("ijk,jy->iyk", plaza_cur, side6), table_height)
        plaza_all = lax.all_gather(plaza_y.reshape(edge, -1), "split", axis=0, tiled=True)
        plaza_all = plaza_all.reshape(plaza_len, 6, height)
        plaza_faces = ein("iyz,ix->yxz", plaza_all, plaza_cols)
        plaza_strips = jnp.concatenate(
            [jnp.zeros_like(plaza_faces), plaza_faces], axis=0
        ).reshape(4, 3, edge, height)
        strips = jnp.concatenate([small_strips, plaza_strips], axis=0)
        segments = strips.reshape(face_count, 3, pieces, seg_cells, height)
        outgoing = ein("sfq,fmqcz->smcz", send_hot, segments)
        arrived = lax.all_to_all(outgoing, "rect", 0, 0, tiled=True)
        remote = ein("fqs,smcz->fmqcz", recv_hot, arrived)
        difference = jnp.where(pair_mask, remote - segments, 0.0)
        layers = interface_layers(difference.reshape(face_count, 3, edge, height))
        small_layers = ein("rz,kz->rk", layers[: owned * 4].reshape(-1, height), table_height)
        small_force = ein("pr,brk->bpk", face_rows, small_layers.reshape(owned, -1, height))
        small_force = small_force.reshape(owned, edge, edge, height)
        plaza_layers = ein("fmxz,kz->xfmk", layers[owned * 4 + 2 :], table_height)
        plaza_gathered = lax.all_gather(plaza_layers.reshape(edge, -1), "split", axis=0, tiled=True)
        plaza_gathered = plaza_gathered.reshape(plaza_len, 6, height)
        plaza_x = ein("xyk,ix->iyk", plaza_gathered, plaza_rows)
        plaza_force = ein("iyk,jy->ijk", plaza_x, side6)
        small_next = small_cos * small_cur - small_old + small_gain * small_force
        plaza_next = plaza_cos * plaza_cur - plaza_old + plaza_gain * plaza_force
        small_old, small_cur = small_cur, small_next
        plaza_old, plaza_cur = plaza_cur, plaza_next
    return (small_cur, small_old, plaza_cur[None], plaza_old[None])


def solution(mesh):
    return jax.shard_map(
        on_device,
        mesh=mesh,
        in_specs=(
            P(("rect", "split"), None, None, None),
            P(("rect", "split"), None, None, None),
            P("rect", "split", None, None),
            P("rect", "split", None, None),
            P("rect", "split", None),
        ),
        out_specs=(
            P(("rect", "split"), None, None, None),
            P(("rect", "split"), None, None, None),
            P("rect", "split", None, None),
            P("rect", "split", None, None),
        ),
        check_vma=False,
    )
```

```python
import jax
import jax.numpy as jnp
from jax import lax
from jax.sharding import PartitionSpec as P

STEPS = 2
COURANT = 0.5
highest = lax.Precision.HIGHEST


def dct_rows_cols(wavenumber, position, length):
    wavenumber = wavenumber.astype(jnp.float32)[:, None]
    position = position.astype(jnp.float32)[None, :]
    weight = jnp.where(wavenumber == 0.0, jnp.sqrt(1.0 / length), jnp.sqrt(2.0 / length))
    return weight * jnp.cos(jnp.pi * wavenumber * (position + 0.5) / length)


def dct_table(length):
    return dct_rows_cols(jnp.arange(length), jnp.arange(length), length)


def update_factors(first_row, row_count, length_x, edge_cells, height_cells):
    wave_x = (first_row + jnp.arange(row_count)).astype(jnp.float32)[:, None, None] / length_x
    wave_y = jnp.arange(edge_cells, dtype=jnp.float32)[None, :, None] / edge_cells
    wave_z = jnp.arange(height_cells, dtype=jnp.float32)[None, None, :] / height_cells
    phase_angle = COURANT * jnp.pi * jnp.sqrt(wave_x**2 + wave_y**2 + wave_z**2)
    twice_cos = 2.0 * jnp.cos(phase_angle)
    forcing_gain = COURANT**2 * jnp.sinc(phase_angle / (2.0 * jnp.pi)) ** 2
    return (twice_cos, forcing_gain)


def interface_layers(difference):
    nearest = difference[:, 0]
    middle = difference[:, 1]
    farthest = difference[:, 2]
    return jnp.stack(
        [
            (270.0 * nearest - 27.0 * middle + 2.0 * farthest) / 180.0,
            (-27.0 * nearest + 2.0 * middle) / 180.0,
            2.0 * nearest / 180.0,
        ],
        axis=1,
    )


def ein(spec, a, b):
    return jnp.einsum(spec, a, b, precision=highest, preferred_element_type=jnp.float32)


def gather_slabs(block):
    count = lax.axis_size("split")
    pieces = [block]
    for shift in range(1, count):
        perm = [(j, (j - shift) % count) for j in range(count)]
        pieces.append(lax.ppermute(block, "split", perm))
    return jnp.concatenate(pieces, axis=0)


def on_device(small_now, small_prev, plaza_now, plaza_prev, face_partner):
    owned = small_now.shape[0]
    edge = small_now.shape[1]
    height = small_now.shape[3]
    slabs = lax.axis_size("split")
    groups = lax.axis_size("rect")
    plaza_len = edge * slabs
    first_row = lax.axis_index("split") * edge

    table_side = dct_table(edge)
    table_height = dct_table(height)
    edge_pos = jnp.array([0, 1, 2, edge - 1, edge - 2, edge - 3], jnp.int32)
    side6 = table_side[:, edge_pos]
    mine = first_row + jnp.arange(edge)
    slab_of = (lax.axis_index("split") + jnp.arange(slabs)) % slabs
    gathered_rows = (slab_of[:, None] * edge + jnp.arange(edge)[None, :]).reshape(-1)
    plaza_cols = dct_rows_cols(gathered_rows, mine, plaza_len)
    plaza_rows = dct_rows_cols(mine, gathered_rows, plaza_len)

    small_cos, small_gain = update_factors(0, edge, edge, edge, height)
    plaza_cos, plaza_gain = update_factors(first_row, edge, plaza_len, edge, height)

    partners = face_partner.reshape(-1)
    seg_count = partners.shape[0]
    face_count = 4 * (owned + 1)
    pieces = seg_count // face_count
    seg_cells = edge // pieces
    unit_count = (2 * owned + 1) * pieces
    slot_most = (unit_count + groups // 2 - 2) // (groups // 2 - 1)
    slots = groups * slot_most
    paired = partners >= 0
    partner_id = jnp.where(paired, partners, 0)
    other_group = partner_id // seg_count
    other_seg = partner_id % seg_count
    same_group = (other_group[:, None] == other_group[None, :]) & paired[:, None] & paired[None, :]
    send_rank = jnp.sum(same_group & (other_seg[None, :] < other_seg[:, None]), axis=1)
    seg_order = jnp.arange(seg_count)
    recv_rank = jnp.sum(same_group & (seg_order[None, :] < seg_order[:, None]), axis=1)
    target = jnp.where(paired, other_group * slot_most + send_rank, -1)
    source = jnp.where(paired, other_group * slot_most + recv_rank, -1)
    slot_ids = jnp.arange(slots)
    send_hot = (slot_ids[:, None] == target[None, :]).astype(jnp.float32)
    send_hot = send_hot.reshape(slots, face_count, pieces)
    recv_hot = (source[:, None] == slot_ids[None, :]).astype(jnp.float32)
    recv_hot = recv_hot.reshape(face_count, pieces, slots)
    pair_mask = paired.reshape(face_count, 1, pieces, 1, 1)

    x_rows = side6[:, None, :, None] * table_side[None, :, None, :]
    y_rows = table_side[:, None, None, :] * side6[None, :, :, None]
    face_rows = jnp.concatenate(
        [x_rows.reshape(edge * edge, 6 * edge), y_rows.reshape(edge * edge, 6 * edge)], axis=1
    )

    small_old, small_cur = small_prev, small_now
    plaza_old, plaza_cur = plaza_prev[0], plaza_now[0]
    for _ in range(STEPS):
        flat_modes = small_cur.reshape(owned, edge * edge, height)
        small_strips = ein("rz,zk->rk", ein("pr,bpk->brk", face_rows, flat_modes).reshape(-1, height), table_height)
        small_strips = small_strips.reshape(owned * 4, 3, edge, height)
        plaza_y = ein("iyk,kz->iyz", ein("ijk,jy->iyk", plaza_cur, side6), table_height)
        plaza_all = gather_slabs(plaza_y.reshape(edge, -1))
        plaza_all = plaza_all.reshape(plaza_len, 6, height)
        plaza_faces = ein("iyz,ix->yxz", plaza_all, plaza_cols)
        plaza_strips = jnp.concatenate(
            [jnp.zeros_like(plaza_faces), plaza_faces], axis=0
        ).reshape(4, 3, edge, height)
        strips = jnp.concatenate([small_strips, plaza_strips], axis=0)
        segments = strips.reshape(face_count, 3, pieces, seg_cells, height)
        outgoing = ein("sfq,fmqcz->smcz", send_hot, segments)
        arrived = lax.all_to_all(outgoing, "rect", 0, 0, tiled=True)
        remote = ein("fqs,smcz->fmqcz", recv_hot, arrived)
        difference = jnp.where(pair_mask, remote - segments, 0.0)
        layers = interface_layers(difference.reshape(face_count, 3, edge, height))
        small_layers = ein("rz,kz->rk", layers[: owned * 4].reshape(-1, height), table_height)
        small_force = ein("pr,brk->bpk", face_rows, small_layers.reshape(owned, -1, height))
        small_force = small_force.reshape(owned, edge, edge, height)
        plaza_layers = ein("fmxz,kz->xfmk", layers[owned * 4 + 2 :], table_height)
        plaza_gathered = gather_slabs(plaza_layers.reshape(edge, -1))
        plaza_gathered = plaza_gathered.reshape(plaza_len, 6, height)
        plaza_x = ein("xyk,ix->iyk", plaza_gathered, plaza_rows)
        plaza_force = ein("iyk,jy->ijk", plaza_x, side6)
        small_next = small_cos * small_cur - small_old + small_gain * small_force
        plaza_next = plaza_cos * plaza_cur - plaza_old + plaza_gain * plaza_force
        small_old, small_cur = small_cur, small_next
        plaza_old, plaza_cur = plaza_cur, plaza_next
    return (small_cur, small_old, plaza_cur[None], plaza_old[None])


def solution(mesh):
    return jax.shard_map(
        on_device,
        mesh=mesh,
        in_specs=(
            P(("rect", "split"), None, None, None),
            P(("rect", "split"), None, None, None),
            P("rect", "split", None, None),
            P("rect", "split", None, None),
            P("rect", "split", None),
        ),
        out_specs=(
            P(("rect", "split"), None, None, None),
            P(("rect", "split"), None, None, None),
            P("rect", "split", None, None),
            P("rect", "split", None, None),
        ),
        check_vma=False,
    )
```

```python
import jax
import jax.numpy as jnp
from jax import lax
from jax.sharding import PartitionSpec as P

STEPS = 2
COURANT = 0.5
highest = lax.Precision.HIGHEST


def dct_rows_cols(wavenumber, position, length):
    wavenumber = wavenumber.astype(jnp.float32)[:, None]
    position = position.astype(jnp.float32)[None, :]
    weight = jnp.where(wavenumber == 0.0, jnp.sqrt(1.0 / length), jnp.sqrt(2.0 / length))
    return weight * jnp.cos(jnp.pi * wavenumber * (position + 0.5) / length)


def dct_table(length):
    return dct_rows_cols(jnp.arange(length), jnp.arange(length), length)


def update_factors(rows, length_x, edge_cells, height_cells):
    wave_x = rows.astype(jnp.float32)[:, None, None] / length_x
    wave_y = jnp.arange(edge_cells, dtype=jnp.float32)[None, :, None] / edge_cells
    wave_z = jnp.arange(height_cells, dtype=jnp.float32)[None, None, :] / height_cells
    phase_angle = COURANT * jnp.pi * jnp.sqrt(wave_x**2 + wave_y**2 + wave_z**2)
    twice_cos = 2.0 * jnp.cos(phase_angle)
    forcing_gain = COURANT**2 * jnp.sinc(phase_angle / (2.0 * jnp.pi)) ** 2
    return (twice_cos, forcing_gain)


def interface_layers(difference):
    nearest = difference[:, 0]
    middle = difference[:, 1]
    farthest = difference[:, 2]
    return jnp.stack(
        [
            (270.0 * nearest - 27.0 * middle + 2.0 * farthest) / 180.0,
            (-27.0 * nearest + 2.0 * middle) / 180.0,
            2.0 * nearest / 180.0,
        ],
        axis=1,
    )


def ein(spec, a, b):
    return jnp.einsum(spec, a, b, precision=highest, preferred_element_type=jnp.float32)


def gather_slabs(block):
    count = lax.axis_size("split")
    pieces = [block]
    for shift in range(1, count):
        perm = [(j, (j - shift) % count) for j in range(count)]
        pieces.append(lax.ppermute(block, "split", perm))
    return jnp.concatenate(pieces, axis=0)


def on_device(small_now, small_prev, plaza_now, plaza_prev, face_partner):
    owned = small_now.shape[0]
    edge = small_now.shape[1]
    height = small_now.shape[3]
    slabs = lax.axis_size("split")
    groups = lax.axis_size("rect")
    plaza_len = edge * slabs
    first_row = lax.axis_index("split") * edge

    table_side = dct_table(edge)
    table_height = dct_table(height)
    edge_pos = jnp.array([0, 1, 2, edge - 1, edge - 2, edge - 3], jnp.int32)
    side6 = table_side[:, edge_pos]
    mine = first_row + jnp.arange(edge)
    slab_of = (lax.axis_index("split") + jnp.arange(slabs)) % slabs
    gathered_rows = (slab_of[:, None] * edge + jnp.arange(edge)[None, :]).reshape(-1)
    plaza_cols = dct_rows_cols(gathered_rows, mine, plaza_len)
    plaza_rows = dct_rows_cols(mine, gathered_rows, plaza_len)
    plaza_square = dct_rows_cols(gathered_rows, gathered_rows, plaza_len)

    small_cos, small_gain = update_factors(jnp.arange(edge), edge, edge, height)
    plaza_cos, plaza_gain = update_factors(mine, plaza_len, edge, height)
    _, gathered_gain = update_factors(gathered_rows, plaza_len, edge, height)

    def project(modes):
        flat = ein("iyk,kz->iyz", ein("ijk,jy->iyk", modes, side6), table_height)
        return flat.reshape(modes.shape[0], -1)

    partners = face_partner.reshape(-1)
    seg_count = partners.shape[0]
    face_count = 4 * (owned + 1)
    pieces = seg_count // face_count
    seg_cells = edge // pieces
    unit_count = (2 * owned + 1) * pieces
    slot_most = (unit_count + groups // 2 - 2) // (groups // 2 - 1)
    slots = groups * slot_most
    paired = partners >= 0
    partner_id = jnp.where(paired, partners, 0)
    other_group = partner_id // seg_count
    other_seg = partner_id % seg_count
    same_group = (other_group[:, None] == other_group[None, :]) & paired[:, None] & paired[None, :]
    send_rank = jnp.sum(same_group & (other_seg[None, :] < other_seg[:, None]), axis=1)
    seg_order = jnp.arange(seg_count)
    recv_rank = jnp.sum(same_group & (seg_order[None, :] < seg_order[:, None]), axis=1)
    target = jnp.where(paired, other_group * slot_most + send_rank, -1)
    source = jnp.where(paired, other_group * slot_most + recv_rank, -1)
    slot_ids = jnp.arange(slots)
    send_hot = (slot_ids[:, None] == target[None, :]).astype(jnp.float32)
    send_hot = send_hot.reshape(slots, face_count, pieces)
    recv_hot = (source[:, None] == slot_ids[None, :]).astype(jnp.float32)
    recv_hot = recv_hot.reshape(face_count, pieces, slots)
    pair_mask = paired.reshape(face_count, 1, pieces, 1, 1)

    x_rows = side6[:, None, :, None] * table_side[None, :, None, :]
    y_rows = table_side[:, None, None, :] * side6[None, :, :, None]
    face_rows = jnp.concatenate(
        [x_rows.reshape(edge * edge, 6 * edge), y_rows.reshape(edge * edge, 6 * edge)], axis=1
    )

    small_old, small_cur = small_prev, small_now
    plaza_old, plaza_cur = plaza_prev[0], plaza_now[0]
    plaza_all = gather_slabs(project(plaza_cur))
    for step in range(STEPS):
        last = step == STEPS - 1
        if not last:
            plaza_ahead = gather_slabs(project(plaza_cos * plaza_cur - plaza_old))
        flat_modes = small_cur.reshape(owned, edge * edge, height)
        small_strips = ein("rz,zk->rk", ein("pr,bpk->brk", face_rows, flat_modes).reshape(-1, height), table_height)
        small_strips = small_strips.reshape(owned * 4, 3, edge, height)
        plaza_faces = ein("iyz,ix->yxz", plaza_all.reshape(plaza_len, 6, height), plaza_cols)
        plaza_strips = jnp.concatenate(
            [jnp.zeros_like(plaza_faces), plaza_faces], axis=0
        ).reshape(4, 3, edge, height)
        strips = jnp.concatenate([small_strips, plaza_strips], axis=0)
        segments = strips.reshape(face_count, 3, pieces, seg_cells, height)
        outgoing = ein("sfq,fmqcz->smcz", send_hot, segments)
        arrived = lax.all_to_all(outgoing, "rect", 0, 0, tiled=True)
        remote = ein("fqs,smcz->fmqcz", recv_hot, arrived)
        difference = jnp.where(pair_mask, remote - segments, 0.0)
        layers = interface_layers(difference.reshape(face_count, 3, edge, height))
        small_layers = ein("rz,kz->rk", layers[: owned * 4].reshape(-1, height), table_height)
        small_force = ein("pr,brk->bpk", face_rows, small_layers.reshape(owned, -1, height))
        small_force = small_force.reshape(owned, edge, edge, height)
        plaza_layers = ein("fmxz,kz->xfmk", layers[owned * 4 + 2 :], table_height)
        plaza_gathered = gather_slabs(plaza_layers.reshape(edge, -1))
        plaza_gathered = plaza_gathered.reshape(plaza_len, 6, height)
        if last:
            plaza_x = ein("xyk,ix->iyk", plaza_gathered, plaza_rows)
            plaza_force = ein("iyk,jy->ijk", plaza_x, side6)
        else:
            every_x = ein("xyk,ix->iyk", plaza_gathered, plaza_square)
            every_force = ein("iyk,jy->ijk", every_x, side6)
            plaza_force = every_force[:edge]
            plaza_all = plaza_ahead + project(gathered_gain * every_force)
        small_next = small_cos * small_cur - small_old + small_gain * small_force
        plaza_next = plaza_cos * plaza_cur - plaza_old + plaza_gain * plaza_force
        small_old, small_cur = small_cur, small_next
        plaza_old, plaza_cur = plaza_cur, plaza_next
    return (small_cur, small_old, plaza_cur[None], plaza_old[None])


def solution(mesh):
    return jax.shard_map(
        on_device,
        mesh=mesh,
        in_specs=(
            P(("rect", "split"), None, None, None),
            P(("rect", "split"), None, None, None),
            P("rect", "split", None, None),
            P("rect", "split", None, None),
            P("rect", "split", None),
        ),
        out_specs=(
            P(("rect", "split"), None, None, None),
            P(("rect", "split"), None, None, None),
            P("rect", "split", None, None),
            P("rect", "split", None, None),
        ),
        check_vma=False,
    )
```

```python
import jax
import jax.numpy as jnp
from jax import lax
from jax.sharding import PartitionSpec as P

STEPS = 2
COURANT = 0.5
highest = lax.Precision.HIGHEST


def dct_rows_cols(wavenumber, position, length):
    wavenumber = wavenumber.astype(jnp.float32)[:, None]
    position = position.astype(jnp.float32)[None, :]
    weight = jnp.where(wavenumber == 0.0, jnp.sqrt(1.0 / length), jnp.sqrt(2.0 / length))
    return weight * jnp.cos(jnp.pi * wavenumber * (position + 0.5) / length)


def dct_table(length):
    return dct_rows_cols(jnp.arange(length), jnp.arange(length), length)


def update_factors(first_row, row_count, length_x, edge_cells, height_cells):
    wave_x = (first_row + jnp.arange(row_count)).astype(jnp.float32)[:, None, None] / length_x
    wave_y = jnp.arange(edge_cells, dtype=jnp.float32)[None, :, None] / edge_cells
    wave_z = jnp.arange(height_cells, dtype=jnp.float32)[None, None, :] / height_cells
    phase_angle = COURANT * jnp.pi * jnp.sqrt(wave_x**2 + wave_y**2 + wave_z**2)
    twice_cos = 2.0 * jnp.cos(phase_angle)
    forcing_gain = COURANT**2 * jnp.sinc(phase_angle / (2.0 * jnp.pi)) ** 2
    return (twice_cos, forcing_gain)


def interface_layers(difference):
    nearest = difference[:, 0]
    middle = difference[:, 1]
    farthest = difference[:, 2]
    return jnp.stack(
        [
            (270.0 * nearest - 27.0 * middle + 2.0 * farthest) / 180.0,
            (-27.0 * nearest + 2.0 * middle) / 180.0,
            2.0 * nearest / 180.0,
        ],
        axis=1,
    )


def ein(spec, a, b):
    return jnp.einsum(spec, a, b, precision=highest, preferred_element_type=jnp.float32)


def gather_slabs(block):
    count = lax.axis_size("split")
    pieces = [block]
    for shift in range(1, count):
        perm = [(j, (j - shift) % count) for j in range(count)]
        pieces.append(lax.ppermute(block, "split", perm))
    return jnp.stack(pieces, axis=0)


def on_device(small_now, small_prev, plaza_now, plaza_prev, face_partner):
    owned = small_now.shape[0]
    edge = small_now.shape[1]
    height = small_now.shape[3]
    slabs = lax.axis_size("split")
    groups = lax.axis_size("rect")
    plaza_len = edge * slabs
    first_row = lax.axis_index("split") * edge

    table_side = dct_table(edge)
    table_height = dct_table(height)
    edge_pos = jnp.array([0, 1, 2, edge - 1, edge - 2, edge - 3], jnp.int32)
    side6 = table_side[:, edge_pos]
    mine = first_row + jnp.arange(edge)
    slab_of = (lax.axis_index("split") + jnp.arange(slabs)) % slabs
    gathered_rows = (slab_of[:, None] * edge + jnp.arange(edge)[None, :]).reshape(-1)
    plaza_cols = dct_rows_cols(gathered_rows, mine, plaza_len)
    plaza_rows = dct_rows_cols(mine, gathered_rows, plaza_len)

    small_cos, small_gain = update_factors(0, edge, edge, edge, height)
    plaza_cos, plaza_gain = update_factors(first_row, edge, plaza_len, edge, height)

    partners = face_partner.reshape(-1)
    seg_count = partners.shape[0]
    face_count = 4 * (owned + 1)
    pieces = seg_count // face_count
    seg_cells = edge // pieces
    unit_count = (2 * owned + 1) * pieces
    slot_most = (unit_count + groups // 2 - 2) // (groups // 2 - 1)
    slots = groups * slot_most
    paired = partners >= 0
    partner_id = jnp.where(paired, partners, 0)
    other_group = partner_id // seg_count
    other_seg = partner_id % seg_count
    same_group = (other_group[:, None] == other_group[None, :]) & paired[:, None] & paired[None, :]
    send_rank = jnp.sum(same_group & (other_seg[None, :] < other_seg[:, None]), axis=1)
    seg_order = jnp.arange(seg_count)
    recv_rank = jnp.sum(same_group & (seg_order[None, :] < seg_order[:, None]), axis=1)
    target = jnp.where(paired, other_group * slot_most + send_rank, -1)
    source = jnp.where(paired, other_group * slot_most + recv_rank, -1)
    slot_ids = jnp.arange(slots)
    send_hot = (slot_ids[:, None] == target[None, :]).astype(jnp.float32)
    send_hot = send_hot.reshape(slots, face_count, pieces)
    recv_hot = (source[:, None] == slot_ids[None, :]).astype(jnp.float32)
    recv_hot = recv_hot.reshape(face_count, pieces, slots)
    pair_mask = paired.reshape(face_count, 1, pieces, 1, 1)

    side_m = side6.reshape(edge, 2, 3)
    piece_cell = table_side.reshape(edge, pieces, seg_cells)
    x_rows = side_m[:, None, :, None, :, None] * piece_cell[None, :, None, :, None, :]
    y_rows = piece_cell[:, None, None, :, None, :] * side_m[None, :, :, None, :, None]
    face_rows = jnp.concatenate(
        [x_rows.reshape(edge * edge, -1), y_rows.reshape(edge * edge, -1)], axis=1
    )
    plaza_cols = plaza_cols.reshape(slabs, edge, pieces, seg_cells)
    plaza_rows = plaza_rows.reshape(edge, slabs, pieces, seg_cells)
    small_segs = owned * 4 * pieces
    seg_size = 3 * seg_cells * height
    send_hot = send_hot.reshape(slots, seg_count)
    recv_hot = recv_hot.reshape(seg_count, slots)
    seg_paired = paired[:, None]

    small_old, small_cur = small_prev, small_now
    plaza_old, plaza_cur = plaza_prev[0], plaza_now[0]
    for _ in range(STEPS):
        small_pre = ein("pr,bpk->brk", face_rows, small_cur.reshape(owned, edge * edge, height))
        plaza_pre = ein("ijk,jy->iyk", plaza_cur, side6)
        inverse = ein(
            "rk,kz->rz",
            jnp.concatenate([small_pre.reshape(-1, height), plaza_pre.reshape(-1, height)], axis=0),
            table_height,
        )
        small_strips = inverse[: owned * 12 * edge].reshape(small_segs, seg_size)
        plaza_y = inverse[owned * 12 * edge :].reshape(edge, 2, 3, height)
        plaza_all = gather_slabs(plaza_y)
        plaza_faces = ein("tismz,tiqc->sqmcz", plaza_all, plaza_cols)
        strips = jnp.concatenate(
            [
                small_strips,
                jnp.zeros((2 * pieces, seg_size), jnp.float32),
                plaza_faces.reshape(2 * pieces, seg_size),
            ],
            axis=0,
        )
        outgoing = ein("se,ed->sd", send_hot, strips)
        arrived = lax.all_to_all(outgoing, "rect", 0, 0, tiled=True)
        remote = ein("es,sd->ed", recv_hot, arrived)
        difference = jnp.where(seg_paired, remote - strips, 0.0)
        layers = interface_layers(difference.reshape(seg_count, 3, seg_cells, height))
        layers_z = ein("rz,kz->rk", layers.reshape(-1, height), table_height)
        layers_z = layers_z.reshape(seg_count, 3, seg_cells, height)
        small_layers = layers_z[:small_segs].reshape(owned, -1, height)
        small_force = ein("pr,brk->bpk", face_rows, small_layers)
        small_force = small_force.reshape(owned, edge, edge, height)
        plaza_layers = layers_z[seg_count - 2 * pieces :].reshape(2, pieces, 3, seg_cells, height)
        plaza_gathered = gather_slabs(plaza_layers)
        plaza_x = ein("tsqmck,itqc->ismk", plaza_gathered, plaza_rows)
        plaza_force = ein("ismk,jsm->ijk", plaza_x, side_m)
        small_next = small_cos * small_cur - small_old + small_gain * small_force
        plaza_next = plaza_cos * plaza_cur - plaza_old + plaza_gain * plaza_force
        small_old, small_cur = small_cur, small_next
        plaza_old, plaza_cur = plaza_cur, plaza_next
    return (small_cur, small_old, plaza_cur[None], plaza_old[None])


def solution(mesh):
    return jax.shard_map(
        on_device,
        mesh=mesh,
        in_specs=(
            P(("rect", "split"), None, None, None),
            P(("rect", "split"), None, None, None),
            P("rect", "split", None, None),
            P("rect", "split", None, None),
            P("rect", "split", None),
        ),
        out_specs=(
            P(("rect", "split"), None, None, None),
            P(("rect", "split"), None, None, None),
            P("rect", "split", None, None),
            P("rect", "split", None, None),
        ),
        check_vma=False,
    )
```

```python
import jax
import jax.numpy as jnp
from jax import lax
from jax.sharding import PartitionSpec as P

STEPS = 2
COURANT = 0.5
highest = lax.Precision.HIGHEST
transform_precision = lax.Precision.HIGH


def dct_rows_cols(wavenumber, position, length):
    wavenumber = wavenumber.astype(jnp.float32)[:, None]
    position = position.astype(jnp.float32)[None, :]
    weight = jnp.where(wavenumber == 0.0, jnp.sqrt(1.0 / length), jnp.sqrt(2.0 / length))
    return weight * jnp.cos(jnp.pi * wavenumber * (position + 0.5) / length)


def dct_table(length):
    return dct_rows_cols(jnp.arange(length), jnp.arange(length), length)


def update_factors(first_row, row_count, length_x, edge_cells, height_cells):
    wave_x = (first_row + jnp.arange(row_count)).astype(jnp.float32)[:, None, None] / length_x
    wave_y = jnp.arange(edge_cells, dtype=jnp.float32)[None, :, None] / edge_cells
    wave_z = jnp.arange(height_cells, dtype=jnp.float32)[None, None, :] / height_cells
    phase_angle = COURANT * jnp.pi * jnp.sqrt(wave_x**2 + wave_y**2 + wave_z**2)
    twice_cos = 2.0 * jnp.cos(phase_angle)
    forcing_gain = COURANT**2 * jnp.sinc(phase_angle / (2.0 * jnp.pi)) ** 2
    return (twice_cos, forcing_gain)


def interface_layers(difference):
    nearest = difference[:, 0]
    middle = difference[:, 1]
    farthest = difference[:, 2]
    return jnp.stack(
        [
            (270.0 * nearest - 27.0 * middle + 2.0 * farthest) / 180.0,
            (-27.0 * nearest + 2.0 * middle) / 180.0,
            2.0 * nearest / 180.0,
        ],
        axis=1,
    )


def ein(spec, a, b, precision=transform_precision):
    return jnp.einsum(spec, a, b, precision=precision, preferred_element_type=jnp.float32)


def gather_slabs(block):
    count = lax.axis_size("split")
    pieces = [block]
    for shift in range(1, count):
        perm = [(j, (j - shift) % count) for j in range(count)]
        pieces.append(lax.ppermute(block, "split", perm))
    return jnp.concatenate(pieces, axis=0)


def on_device(small_now, small_prev, plaza_now, plaza_prev, face_partner):
    owned = small_now.shape[0]
    edge = small_now.shape[1]
    height = small_now.shape[3]
    slabs = lax.axis_size("split")
    groups = lax.axis_size("rect")
    plaza_len = edge * slabs
    first_row = lax.axis_index("split") * edge

    table_side = dct_table(edge)
    table_height = dct_table(height)
    edge_pos = jnp.array([0, 1, 2, edge - 1, edge - 2, edge - 3], jnp.int32)
    side6 = table_side[:, edge_pos]
    mine = first_row + jnp.arange(edge)
    slab_of = (lax.axis_index("split") + jnp.arange(slabs)) % slabs
    gathered_rows = (slab_of[:, None] * edge + jnp.arange(edge)[None, :]).reshape(-1)
    plaza_cols = dct_rows_cols(gathered_rows, mine, plaza_len)
    plaza_rows = dct_rows_cols(mine, gathered_rows, plaza_len)

    small_cos, small_gain = update_factors(0, edge, edge, edge, height)
    plaza_cos, plaza_gain = update_factors(first_row, edge, plaza_len, edge, height)

    partners = face_partner.reshape(-1)
    seg_count = partners.shape[0]
    face_count = 4 * (owned + 1)
    pieces = seg_count // face_count
    seg_cells = edge // pieces
    unit_count = (2 * owned + 1) * pieces
    slot_most = (unit_count + groups // 2 - 2) // (groups // 2 - 1)
    slots = groups * slot_most
    paired = partners >= 0
    partner_id = jnp.where(paired, partners, 0)
    other_group = partner_id // seg_count
    other_seg = partner_id % seg_count
    same_group = (other_group[:, None] == other_group[None, :]) & paired[:, None] & paired[None, :]
    send_rank = jnp.sum(same_group & (other_seg[None, :] < other_seg[:, None]), axis=1)
    seg_order = jnp.arange(seg_count)
    recv_rank = jnp.sum(same_group & (seg_order[None, :] < seg_order[:, None]), axis=1)
    target = jnp.where(paired, other_group * slot_most + send_rank, -1)
    source = jnp.where(paired, other_group * slot_most + recv_rank, -1)
    slot_ids = jnp.arange(slots)
    send_hot = (slot_ids[:, None] == target[None, :]).astype(jnp.float32)
    send_hot = send_hot.reshape(slots, face_count, pieces)
    recv_hot = (source[:, None] == slot_ids[None, :]).astype(jnp.float32)
    recv_hot = recv_hot.reshape(face_count, pieces, slots)
    pair_mask = paired.reshape(face_count, 1, pieces, 1, 1)

    x_rows = side6[:, None, :, None] * table_side[None, :, None, :]
    y_rows = table_side[:, None, None, :] * side6[None, :, :, None]
    face_rows = jnp.concatenate(
        [x_rows.reshape(edge * edge, 6 * edge), y_rows.reshape(edge * edge, 6 * edge)], axis=1
    )

    small_old, small_cur = small_prev, small_now
    plaza_old, plaza_cur = plaza_prev[0], plaza_now[0]
    for _ in range(STEPS):
        flat_modes = small_cur.reshape(owned, edge * edge, height)
        small_strips = ein("rz,zk->rk", ein("pr,bpk->brk", face_rows, flat_modes).reshape(-1, height), table_height)
        small_strips = small_strips.reshape(owned * 4, 3, edge, height)
        plaza_y = ein("iyk,kz->iyz", ein("ijk,jy->iyk", plaza_cur, side6), table_height)
        plaza_all = gather_slabs(plaza_y.reshape(edge, -1))
        plaza_all = plaza_all.reshape(plaza_len, 6, height)
        plaza_faces = ein("iyz,ix->yxz", plaza_all, plaza_cols)
        plaza_strips = jnp.concatenate(
            [jnp.zeros_like(plaza_faces), plaza_faces], axis=0
        ).reshape(4, 3, edge, height)
        strips = jnp.concatenate([small_strips, plaza_strips], axis=0)
        segments = strips.reshape(face_count, 3, pieces, seg_cells, height)
        outgoing = ein("sfq,fmqcz->smcz", send_hot, segments, highest)
        arrived = lax.all_to_all(outgoing, "rect", 0, 0, tiled=True)
        remote = ein("fqs,smcz->fmqcz", recv_hot, arrived, highest)
        difference = jnp.where(pair_mask, remote - segments, 0.0)
        layers = interface_layers(difference.reshape(face_count, 3, edge, height))
        small_layers = ein("rz,kz->rk", layers[: owned * 4].reshape(-1, height), table_height)
        small_force = ein("pr,brk->bpk", face_rows, small_layers.reshape(owned, -1, height))
        small_force = small_force.reshape(owned, edge, edge, height)
        plaza_layers = ein("fmxz,kz->xfmk", layers[owned * 4 + 2 :], table_height)
        plaza_gathered = gather_slabs(plaza_layers.reshape(edge, -1))
        plaza_gathered = plaza_gathered.reshape(plaza_len, 6, height)
        plaza_x = ein("xyk,ix->iyk", plaza_gathered, plaza_rows)
        plaza_force = ein("iyk,jy->ijk", plaza_x, side6)
        small_next = small_cos * small_cur - small_old + small_gain * small_force
        plaza_next = plaza_cos * plaza_cur - plaza_old + plaza_gain * plaza_force
        small_old, small_cur = small_cur, small_next
        plaza_old, plaza_cur = plaza_cur, plaza_next
    return (small_cur, small_old, plaza_cur[None], plaza_old[None])


def solution(mesh):
    return jax.shard_map(
        on_device,
        mesh=mesh,
        in_specs=(
            P(("rect", "split"), None, None, None),
            P(("rect", "split"), None, None, None),
            P("rect", "split", None, None),
            P("rect", "split", None, None),
            P("rect", "split", None),
        ),
        out_specs=(
            P(("rect", "split"), None, None, None),
            P(("rect", "split"), None, None, None),
            P("rect", "split", None, None),
            P("rect", "split", None, None),
        ),
        check_vma=False,
    )
```

```python
import jax
import jax.numpy as jnp
from jax import lax
from jax.sharding import PartitionSpec as P

STEPS = 2
COURANT = 0.5
highest = lax.Precision.HIGHEST


def dct_rows_cols(wavenumber, position, length):
    wavenumber = wavenumber.astype(jnp.float32)[:, None]
    position = position.astype(jnp.float32)[None, :]
    weight = jnp.where(wavenumber == 0.0, jnp.sqrt(1.0 / length), jnp.sqrt(2.0 / length))
    return weight * jnp.cos(jnp.pi * wavenumber * (position + 0.5) / length)


def dct_table(length):
    return dct_rows_cols(jnp.arange(length), jnp.arange(length), length)


def update_factors(first_row, row_count, length_x, edge_cells, height_cells):
    wave_x = (first_row + jnp.arange(row_count)).astype(jnp.float32)[:, None, None] / length_x
    wave_y = jnp.arange(edge_cells, dtype=jnp.float32)[None, :, None] / edge_cells
    wave_z = jnp.arange(height_cells, dtype=jnp.float32)[None, None, :] / height_cells
    phase_angle = COURANT * jnp.pi * jnp.sqrt(wave_x**2 + wave_y**2 + wave_z**2)
    twice_cos = 2.0 * jnp.cos(phase_angle)
    forcing_gain = COURANT**2 * jnp.sinc(phase_angle / (2.0 * jnp.pi)) ** 2
    return (twice_cos, forcing_gain)


def interface_layers(difference):
    nearest = difference[:, 0]
    middle = difference[:, 1]
    farthest = difference[:, 2]
    return jnp.stack(
        [
            (270.0 * nearest - 27.0 * middle + 2.0 * farthest) / 180.0,
            (-27.0 * nearest + 2.0 * middle) / 180.0,
            2.0 * nearest / 180.0,
        ],
        axis=1,
    )


def ein(spec, a, b):
    return jnp.einsum(spec, a, b, precision=highest, preferred_element_type=jnp.float32)


def gather_slabs(block):
    count = lax.axis_size("split")
    pieces = [block]
    for shift in range(1, count):
        perm = [(j, (j - shift) % count) for j in range(count)]
        pieces.append(lax.ppermute(block, "split", perm))
    return jnp.concatenate(pieces, axis=0)


def on_device(small_now, small_prev, plaza_now, plaza_prev, face_partner):
    owned = small_now.shape[0]
    edge = small_now.shape[1]
    height = small_now.shape[3]
    slabs = lax.axis_size("split")
    groups = lax.axis_size("rect")
    plaza_len = edge * slabs
    first_row = lax.axis_index("split") * edge

    table_side = dct_table(edge)
    table_height = dct_table(height)
    edge_pos = jnp.array([0, 1, 2, edge - 1, edge - 2, edge - 3], jnp.int32)
    side6 = table_side[:, edge_pos]
    mine = first_row + jnp.arange(edge)
    slab_of = (lax.axis_index("split") + jnp.arange(slabs)) % slabs
    gathered_rows = (slab_of[:, None] * edge + jnp.arange(edge)[None, :]).reshape(-1)
    plaza_cols = dct_rows_cols(gathered_rows, mine, plaza_len)
    plaza_rows = dct_rows_cols(mine, gathered_rows, plaza_len)

    small_cos, small_gain = update_factors(0, edge, edge, edge, height)
    plaza_cos, plaza_gain = update_factors(first_row, edge, plaza_len, edge, height)

    partners = face_partner.reshape(-1)
    seg_count = partners.shape[0]
    face_count = 4 * (owned + 1)
    pieces = seg_count // face_count
    seg_cells = edge // pieces
    unit_count = (2 * owned + 1) * pieces
    slot_most = (unit_count + groups // 2 - 2) // (groups // 2 - 1)
    slots = groups * slot_most
    paired = partners >= 0
    partner_id = jnp.where(paired, partners, 0)
    other_group = partner_id // seg_count
    other_seg = partner_id % seg_count
    same_group = (other_group[:, None] == other_group[None, :]) & paired[:, None] & paired[None, :]
    send_rank = jnp.sum(same_group & (other_seg[None, :] < other_seg[:, None]), axis=1)
    seg_order = jnp.arange(seg_count)
    recv_rank = jnp.sum(same_group & (seg_order[None, :] < seg_order[:, None]), axis=1)
    target = jnp.where(paired, other_group * slot_most + send_rank, -1)
    source = jnp.where(paired, other_group * slot_most + recv_rank, -1)
    slot_ids = jnp.arange(slots)
    send_hot = (slot_ids[:, None] == target[None, :]).astype(jnp.float32)
    send_hot = send_hot.reshape(slots, face_count, pieces)
    recv_hot = (source[:, None] == slot_ids[None, :]).astype(jnp.float32)
    recv_hot = recv_hot.reshape(face_count, pieces, slots)
    pair_mask = paired.reshape(face_count, 1, pieces, 1, 1)

    x_rows = side6[:, None, :, None] * table_side[None, :, None, :]
    y_rows = table_side[:, None, None, :] * side6[None, :, :, None]
    face_rows = jnp.concatenate(
        [x_rows.reshape(edge * edge, 6 * edge), y_rows.reshape(edge * edge, 6 * edge)], axis=1
    )

    small_old, small_cur = small_prev, small_now
    plaza_old, plaza_cur = plaza_prev[0], plaza_now[0]
    for _ in range(STEPS):
        flat_modes = small_cur.reshape(owned, edge * edge, height)
        small_pre = ein("pr,bpk->brk", face_rows, flat_modes).reshape(-1, height)
        plaza_pre = ein("ijk,jy->iyk", plaza_cur, side6).reshape(-1, height)
        inverse = ein("rk,kz->rz", jnp.concatenate([small_pre, plaza_pre], axis=0), table_height)
        small_strips = inverse[: small_pre.shape[0]].reshape(owned * 4, 3, edge, height)
        plaza_y = inverse[small_pre.shape[0] :]
        plaza_all = gather_slabs(plaza_y.reshape(edge, -1))
        plaza_all = plaza_all.reshape(plaza_len, 6, height)
        plaza_faces = ein("iyz,ix->yxz", plaza_all, plaza_cols)
        plaza_strips = jnp.concatenate(
            [jnp.zeros_like(plaza_faces), plaza_faces], axis=0
        ).reshape(4, 3, edge, height)
        strips = jnp.concatenate([small_strips, plaza_strips], axis=0)
        segments = strips.reshape(face_count, 3, pieces, seg_cells, height)
        outgoing = ein("sfq,fmqcz->smcz", send_hot, segments)
        arrived = lax.all_to_all(outgoing, "rect", 0, 0, tiled=True)
        remote = ein("fqs,smcz->fmqcz", recv_hot, arrived)
        difference = jnp.where(pair_mask, remote - segments, 0.0)
        layers = interface_layers(difference.reshape(face_count, 3, edge, height))
        layers_z = ein("rz,kz->rk", layers.reshape(-1, height), table_height)
        layers_z = layers_z.reshape(face_count, 3, edge, height)
        small_layers = layers_z[: owned * 4].reshape(-1, height)
        small_force = ein("pr,brk->bpk", face_rows, small_layers.reshape(owned, -1, height))
        small_force = small_force.reshape(owned, edge, edge, height)
        plaza_layers = jnp.transpose(layers_z[owned * 4 + 2 :], (2, 0, 1, 3))
        plaza_gathered = gather_slabs(plaza_layers.reshape(edge, -1))
        plaza_gathered = plaza_gathered.reshape(plaza_len, 6, height)
        plaza_x = ein("xyk,ix->iyk", plaza_gathered, plaza_rows)
        plaza_force = ein("iyk,jy->ijk", plaza_x, side6)
        small_next = small_cos * small_cur - small_old + small_gain * small_force
        plaza_next = plaza_cos * plaza_cur - plaza_old + plaza_gain * plaza_force
        small_old, small_cur = small_cur, small_next
        plaza_old, plaza_cur = plaza_cur, plaza_next
    return (small_cur, small_old, plaza_cur[None], plaza_old[None])


def solution(mesh):
    return jax.shard_map(
        on_device,
        mesh=mesh,
        in_specs=(
            P(("rect", "split"), None, None, None),
            P(("rect", "split"), None, None, None),
            P("rect", "split", None, None),
            P("rect", "split", None, None),
            P("rect", "split", None),
        ),
        out_specs=(
            P(("rect", "split"), None, None, None),
            P(("rect", "split"), None, None, None),
            P("rect", "split", None, None),
            P("rect", "split", None, None),
        ),
        check_vma=False,
    )
```

```python
import jax
import jax.numpy as jnp
from jax import lax
from jax.sharding import PartitionSpec as P

STEPS = 2
COURANT = 0.5
highest = lax.Precision.HIGHEST


def dct_rows_cols(wavenumber, position, length):
    wavenumber = wavenumber.astype(jnp.float32)[:, None]
    position = position.astype(jnp.float32)[None, :]
    weight = jnp.where(wavenumber == 0.0, jnp.sqrt(1.0 / length), jnp.sqrt(2.0 / length))
    return weight * jnp.cos(jnp.pi * wavenumber * (position + 0.5) / length)


def dct_table(length):
    return dct_rows_cols(jnp.arange(length), jnp.arange(length), length)


def update_factors(first_row, row_count, length_x, edge_cells, height_cells):
    wave_x = (first_row + jnp.arange(row_count)).astype(jnp.float32)[:, None, None] / length_x
    wave_y = jnp.arange(edge_cells, dtype=jnp.float32)[None, :, None] / edge_cells
    wave_z = jnp.arange(height_cells, dtype=jnp.float32)[None, None, :] / height_cells
    phase_angle = COURANT * jnp.pi * jnp.sqrt(wave_x**2 + wave_y**2 + wave_z**2)
    twice_cos = 2.0 * jnp.cos(phase_angle)
    forcing_gain = COURANT**2 * jnp.sinc(phase_angle / (2.0 * jnp.pi)) ** 2
    return (twice_cos, forcing_gain)


def interface_layers(difference):
    nearest = difference[:, 0]
    middle = difference[:, 1]
    farthest = difference[:, 2]
    return jnp.stack(
        [
            (270.0 * nearest - 27.0 * middle + 2.0 * farthest) / 180.0,
            (-27.0 * nearest + 2.0 * middle) / 180.0,
            2.0 * nearest / 180.0,
        ],
        axis=1,
    )


def ein(spec, a, b):
    return jnp.einsum(spec, a, b, precision=highest, preferred_element_type=jnp.float32)


def sum_from_slabs(parts):
    count = lax.axis_size("split")
    total = parts[0]
    for shift in range(1, count):
        perm = [(j, (j + shift) % count) for j in range(count)]
        total = total + lax.ppermute(parts[shift], "split", perm)
    return total


def gather_slabs(block):
    count = lax.axis_size("split")
    pieces = [block]
    for shift in range(1, count):
        perm = [(j, (j - shift) % count) for j in range(count)]
        pieces.append(lax.ppermute(block, "split", perm))
    return jnp.concatenate(pieces, axis=0)


def on_device(small_now, small_prev, plaza_now, plaza_prev, face_partner):
    owned = small_now.shape[0]
    edge = small_now.shape[1]
    height = small_now.shape[3]
    slabs = lax.axis_size("split")
    groups = lax.axis_size("rect")
    plaza_len = edge * slabs
    first_row = lax.axis_index("split") * edge

    table_side = dct_table(edge)
    table_height = dct_table(height)
    edge_pos = jnp.array([0, 1, 2, edge - 1, edge - 2, edge - 3], jnp.int32)
    side6 = table_side[:, edge_pos]
    mine = first_row + jnp.arange(edge)
    slab_of = (lax.axis_index("split") + jnp.arange(slabs)) % slabs
    gathered_rows = (slab_of[:, None] * edge + jnp.arange(edge)[None, :]).reshape(-1)
    plaza_cols = dct_rows_cols(gathered_rows, mine, plaza_len)
    plaza_rows = dct_rows_cols(mine, gathered_rows, plaza_len)

    small_cos, small_gain = update_factors(0, edge, edge, edge, height)
    plaza_cos, plaza_gain = update_factors(first_row, edge, plaza_len, edge, height)

    partners = face_partner.reshape(-1)
    seg_count = partners.shape[0]
    face_count = 4 * (owned + 1)
    pieces = seg_count // face_count
    seg_cells = edge // pieces
    unit_count = (2 * owned + 1) * pieces
    slot_most = (unit_count + groups // 2 - 2) // (groups // 2 - 1)
    slots = groups * slot_most
    paired = partners >= 0
    partner_id = jnp.where(paired, partners, 0)
    other_group = partner_id // seg_count
    other_seg = partner_id % seg_count
    same_group = (other_group[:, None] == other_group[None, :]) & paired[:, None] & paired[None, :]
    send_rank = jnp.sum(same_group & (other_seg[None, :] < other_seg[:, None]), axis=1)
    seg_order = jnp.arange(seg_count)
    recv_rank = jnp.sum(same_group & (seg_order[None, :] < seg_order[:, None]), axis=1)
    target = jnp.where(paired, other_group * slot_most + send_rank, -1)
    source = jnp.where(paired, other_group * slot_most + recv_rank, -1)
    slot_ids = jnp.arange(slots)
    send_hot = (slot_ids[:, None] == target[None, :]).astype(jnp.float32)
    send_hot = send_hot.reshape(slots, face_count, pieces)
    recv_hot = (source[:, None] == slot_ids[None, :]).astype(jnp.float32)
    recv_hot = recv_hot.reshape(face_count, pieces, slots)
    pair_mask = paired.reshape(face_count, 1, pieces, 1, 1)

    x_rows = side6[:, None, :, None] * table_side[None, :, None, :]
    y_rows = table_side[:, None, None, :] * side6[None, :, :, None]
    face_rows = jnp.concatenate(
        [x_rows.reshape(edge * edge, 6 * edge), y_rows.reshape(edge * edge, 6 * edge)], axis=1
    )

    small_old, small_cur = small_prev, small_now
    plaza_old, plaza_cur = plaza_prev[0], plaza_now[0]
    for _ in range(STEPS):
        flat_modes = small_cur.reshape(owned, edge * edge, height)
        small_strips = ein("rz,zk->rk", ein("pr,bpk->brk", face_rows, flat_modes).reshape(-1, height), table_height)
        small_strips = small_strips.reshape(owned * 4, 3, edge, height)
        plaza_y = ein("iyk,kz->iyz", ein("ijk,jy->iyk", plaza_cur, side6), table_height)
        plaza_shares = ein("ix,id->xd", plaza_rows, plaza_y.reshape(edge, -1))
        plaza_faces = sum_from_slabs(plaza_shares.reshape(slabs, edge, -1))
        plaza_faces = jnp.swapaxes(plaza_faces.reshape(edge, 6, height), 0, 1)
        plaza_strips = jnp.concatenate(
            [jnp.zeros_like(plaza_faces), plaza_faces], axis=0
        ).reshape(4, 3, edge, height)
        strips = jnp.concatenate([small_strips, plaza_strips], axis=0)
        segments = strips.reshape(face_count, 3, pieces, seg_cells, height)
        outgoing = ein("sfq,fmqcz->smcz", send_hot, segments)
        arrived = lax.all_to_all(outgoing, "rect", 0, 0, tiled=True)
        remote = ein("fqs,smcz->fmqcz", recv_hot, arrived)
        difference = jnp.where(pair_mask, remote - segments, 0.0)
        layers = interface_layers(difference.reshape(face_count, 3, edge, height))
        small_layers = ein("rz,kz->rk", layers[: owned * 4].reshape(-1, height), table_height)
        small_force = ein("pr,brk->bpk", face_rows, small_layers.reshape(owned, -1, height))
        small_force = small_force.reshape(owned, edge, edge, height)
        plaza_layers = ein("fmxz,kz->xfmk", layers[owned * 4 + 2 :], table_height)
        force_shares = ein("ix,xd->id", plaza_cols, plaza_layers.reshape(edge, -1))
        plaza_x = sum_from_slabs(force_shares.reshape(slabs, edge, -1)).reshape(edge, 6, height)
        plaza_force = ein("iyk,jy->ijk", plaza_x, side6)
        small_next = small_cos * small_cur - small_old + small_gain * small_force
        plaza_next = plaza_cos * plaza_cur - plaza_old + plaza_gain * plaza_force
        small_old, small_cur = small_cur, small_next
        plaza_old, plaza_cur = plaza_cur, plaza_next
    return (small_cur, small_old, plaza_cur[None], plaza_old[None])


def solution(mesh):
    return jax.shard_map(
        on_device,
        mesh=mesh,
        in_specs=(
            P(("rect", "split"), None, None, None),
            P(("rect", "split"), None, None, None),
            P("rect", "split", None, None),
            P("rect", "split", None, None),
            P("rect", "split", None),
        ),
        out_specs=(
            P(("rect", "split"), None, None, None),
            P(("rect", "split"), None, None, None),
            P("rect", "split", None, None),
            P("rect", "split", None, None),
        ),
        check_vma=False,
    )
```

```python
import jax
import jax.numpy as jnp
from jax import lax
from jax.sharding import PartitionSpec as P

STEPS = 2
COURANT = 0.5
highest = lax.Precision.HIGHEST


def dct_rows_cols(wavenumber, position, length):
    wavenumber = wavenumber.astype(jnp.float32)[:, None]
    position = position.astype(jnp.float32)[None, :]
    weight = jnp.where(wavenumber == 0.0, jnp.sqrt(1.0 / length), jnp.sqrt(2.0 / length))
    return weight * jnp.cos(jnp.pi * wavenumber * (position + 0.5) / length)


def dct_table(length):
    return dct_rows_cols(jnp.arange(length), jnp.arange(length), length)


def update_factors(first_row, row_count, length_x, edge_cells, height_cells):
    wave_x = (first_row + jnp.arange(row_count)).astype(jnp.float32)[:, None, None] / length_x
    wave_y = jnp.arange(edge_cells, dtype=jnp.float32)[None, :, None] / edge_cells
    wave_z = jnp.arange(height_cells, dtype=jnp.float32)[None, None, :] / height_cells
    phase_angle = COURANT * jnp.pi * jnp.sqrt(wave_x**2 + wave_y**2 + wave_z**2)
    twice_cos = 2.0 * jnp.cos(phase_angle)
    forcing_gain = COURANT**2 * jnp.sinc(phase_angle / (2.0 * jnp.pi)) ** 2
    return (twice_cos, forcing_gain)


def interface_layers(difference):
    nearest = difference[:, 0]
    middle = difference[:, 1]
    farthest = difference[:, 2]
    return jnp.stack(
        [
            (270.0 * nearest - 27.0 * middle + 2.0 * farthest) / 180.0,
            (-27.0 * nearest + 2.0 * middle) / 180.0,
            2.0 * nearest / 180.0,
        ],
        axis=1,
    )


def ein(spec, a, b):
    return jnp.einsum(spec, a, b, precision=highest, preferred_element_type=jnp.float32)


def gather_slabs(block):
    count = lax.axis_size("split")
    copies = jnp.broadcast_to(block[None], (count,) + block.shape)
    return lax.all_to_all(copies, "split", 0, 0, tiled=True).reshape(-1, block.shape[-1])


def on_device(small_now, small_prev, plaza_now, plaza_prev, face_partner):
    owned = small_now.shape[0]
    edge = small_now.shape[1]
    height = small_now.shape[3]
    slabs = lax.axis_size("split")
    groups = lax.axis_size("rect")
    plaza_len = edge * slabs
    first_row = lax.axis_index("split") * edge

    table_side = dct_table(edge)
    table_height = dct_table(height)
    edge_pos = jnp.array([0, 1, 2, edge - 1, edge - 2, edge - 3], jnp.int32)
    side6 = table_side[:, edge_pos]
    mine = first_row + jnp.arange(edge)
    gathered_rows = jnp.arange(plaza_len)
    plaza_cols = dct_rows_cols(gathered_rows, mine, plaza_len)
    plaza_rows = dct_rows_cols(mine, gathered_rows, plaza_len)

    small_cos, small_gain = update_factors(0, edge, edge, edge, height)
    plaza_cos, plaza_gain = update_factors(first_row, edge, plaza_len, edge, height)

    partners = face_partner.reshape(-1)
    seg_count = partners.shape[0]
    face_count = 4 * (owned + 1)
    pieces = seg_count // face_count
    seg_cells = edge // pieces
    unit_count = (2 * owned + 1) * pieces
    slot_most = (unit_count + groups // 2 - 2) // (groups // 2 - 1)
    slots = groups * slot_most
    paired = partners >= 0
    partner_id = jnp.where(paired, partners, 0)
    other_group = partner_id // seg_count
    other_seg = partner_id % seg_count
    same_group = (other_group[:, None] == other_group[None, :]) & paired[:, None] & paired[None, :]
    send_rank = jnp.sum(same_group & (other_seg[None, :] < other_seg[:, None]), axis=1)
    seg_order = jnp.arange(seg_count)
    recv_rank = jnp.sum(same_group & (seg_order[None, :] < seg_order[:, None]), axis=1)
    target = jnp.where(paired, other_group * slot_most + send_rank, -1)
    source = jnp.where(paired, other_group * slot_most + recv_rank, -1)
    slot_ids = jnp.arange(slots)
    send_hot = (slot_ids[:, None] == target[None, :]).astype(jnp.float32)
    send_hot = send_hot.reshape(slots, face_count, pieces)
    recv_hot = (source[:, None] == slot_ids[None, :]).astype(jnp.float32)
    recv_hot = recv_hot.reshape(face_count, pieces, slots)
    pair_mask = paired.reshape(face_count, 1, pieces, 1, 1)

    x_rows = side6[:, None, :, None] * table_side[None, :, None, :]
    y_rows = table_side[:, None, None, :] * side6[None, :, :, None]
    face_rows = jnp.concatenate(
        [x_rows.reshape(edge * edge, 6 * edge), y_rows.reshape(edge * edge, 6 * edge)], axis=1
    )

    small_old, small_cur = small_prev, small_now
    plaza_old, plaza_cur = plaza_prev[0], plaza_now[0]
    for _ in range(STEPS):
        flat_modes = small_cur.reshape(owned, edge * edge, height)
        small_strips = ein("rz,zk->rk", ein("pr,bpk->brk", face_rows, flat_modes).reshape(-1, height), table_height)
        small_strips = small_strips.reshape(owned * 4, 3, edge, height)
        plaza_y = ein("iyk,kz->iyz", ein("ijk,jy->iyk", plaza_cur, side6), table_height)
        plaza_all = gather_slabs(plaza_y.reshape(edge, -1))
        plaza_all = plaza_all.reshape(plaza_len, 6, height)
        plaza_faces = ein("iyz,ix->yxz", plaza_all, plaza_cols)
        plaza_strips = jnp.concatenate(
            [jnp.zeros_like(plaza_faces), plaza_faces], axis=0
        ).reshape(4, 3, edge, height)
        strips = jnp.concatenate([small_strips, plaza_strips], axis=0)
        segments = strips.reshape(face_count, 3, pieces, seg_cells, height)
        outgoing = ein("sfq,fmqcz->smcz", send_hot, segments)
        arrived = lax.all_to_all(outgoing, "rect", 0, 0, tiled=True)
        remote = ein("fqs,smcz->fmqcz", recv_hot, arrived)
        difference = jnp.where(pair_mask, remote - segments, 0.0)
        layers = interface_layers(difference.reshape(face_count, 3, edge, height))
        small_layers = ein("rz,kz->rk", layers[: owned * 4].reshape(-1, height), table_height)
        small_force = ein("pr,brk->bpk", face_rows, small_layers.reshape(owned, -1, height))
        small_force = small_force.reshape(owned, edge, edge, height)
        plaza_layers = ein("fmxz,kz->xfmk", layers[owned * 4 + 2 :], table_height)
        plaza_gathered = gather_slabs(plaza_layers.reshape(edge, -1))
        plaza_gathered = plaza_gathered.reshape(plaza_len, 6, height)
        plaza_x = ein("xyk,ix->iyk", plaza_gathered, plaza_rows)
        plaza_force = ein("iyk,jy->ijk", plaza_x, side6)
        small_next = small_cos * small_cur - small_old + small_gain * small_force
        plaza_next = plaza_cos * plaza_cur - plaza_old + plaza_gain * plaza_force
        small_old, small_cur = small_cur, small_next
        plaza_old, plaza_cur = plaza_cur, plaza_next
    return (small_cur, small_old, plaza_cur[None], plaza_old[None])


def solution(mesh):
    return jax.shard_map(
        on_device,
        mesh=mesh,
        in_specs=(
            P(("rect", "split"), None, None, None),
            P(("rect", "split"), None, None, None),
            P("rect", "split", None, None),
            P("rect", "split", None, None),
            P("rect", "split", None),
        ),
        out_specs=(
            P(("rect", "split"), None, None, None),
            P(("rect", "split"), None, None, None),
            P("rect", "split", None, None),
            P("rect", "split", None, None),
        ),
        check_vma=False,
    )
```

```python
import jax
import jax.numpy as jnp
from jax import lax
from jax.sharding import PartitionSpec as P

STEPS = 2
COURANT = 0.5
highest = lax.Precision.HIGHEST


def dct_rows_cols(wavenumber, position, length):
    wavenumber = wavenumber.astype(jnp.float32)[:, None]
    position = position.astype(jnp.float32)[None, :]
    weight = jnp.where(wavenumber == 0.0, jnp.sqrt(1.0 / length), jnp.sqrt(2.0 / length))
    return weight * jnp.cos(jnp.pi * wavenumber * (position + 0.5) / length)


def dct_table(length):
    return dct_rows_cols(jnp.arange(length), jnp.arange(length), length)


def update_factors(first_row, row_count, length_x, edge_cells, height_cells):
    wave_x = (first_row + jnp.arange(row_count)).astype(jnp.float32)[:, None, None] / length_x
    wave_y = jnp.arange(edge_cells, dtype=jnp.float32)[None, :, None] / edge_cells
    wave_z = jnp.arange(height_cells, dtype=jnp.float32)[None, None, :] / height_cells
    phase_angle = COURANT * jnp.pi * jnp.sqrt(wave_x**2 + wave_y**2 + wave_z**2)
    twice_cos = 2.0 * jnp.cos(phase_angle)
    forcing_gain = COURANT**2 * jnp.sinc(phase_angle / (2.0 * jnp.pi)) ** 2
    return (twice_cos, forcing_gain)


def interface_layers(difference):
    nearest = difference[:, 0]
    middle = difference[:, 1]
    farthest = difference[:, 2]
    return jnp.stack(
        [
            (270.0 * nearest - 27.0 * middle + 2.0 * farthest) / 180.0,
            (-27.0 * nearest + 2.0 * middle) / 180.0,
            2.0 * nearest / 180.0,
        ],
        axis=1,
    )


def ein(spec, a, b):
    return jnp.einsum(spec, a, b, precision=highest, preferred_element_type=jnp.float32)


def gather_slabs(block):
    count = lax.axis_size("split")
    pieces = [block]
    for shift in range(1, count):
        perm = [(j, (j - shift) % count) for j in range(count)]
        pieces.append(lax.ppermute(block, "split", perm))
    return jnp.concatenate(pieces, axis=0)


def on_device(small_now, small_prev, plaza_now, plaza_prev, face_partner):
    owned = small_now.shape[0]
    edge = small_now.shape[1]
    height = small_now.shape[3]
    slabs = lax.axis_size("split")
    groups = lax.axis_size("rect")
    plaza_len = edge * slabs
    first_row = lax.axis_index("split") * edge

    table_side = dct_table(edge)
    table_height = dct_table(height)
    edge_pos = jnp.array([0, 1, 2, edge - 1, edge - 2, edge - 3], jnp.int32)
    side6 = table_side[:, edge_pos]
    mine = first_row + jnp.arange(edge)
    slab_of = (lax.axis_index("split") + jnp.arange(slabs)) % slabs
    gathered_rows = (slab_of[:, None] * edge + jnp.arange(edge)[None, :]).reshape(-1)
    plaza_cols = dct_rows_cols(gathered_rows, mine, plaza_len)
    plaza_rows = dct_rows_cols(mine, gathered_rows, plaza_len)

    small_cos, small_gain = update_factors(0, edge, edge, edge, height)
    plaza_cos, plaza_gain = update_factors(first_row, edge, plaza_len, edge, height)

    partners = face_partner.reshape(-1)
    seg_count = partners.shape[0]
    face_count = 4 * (owned + 1)
    pieces = seg_count // face_count
    seg_cells = edge // pieces
    unit_count = (2 * owned + 1) * pieces
    slot_most = (unit_count + groups // 2 - 2) // (groups // 2 - 1)
    slots = groups * slot_most
    paired = partners >= 0
    partner_id = jnp.where(paired, partners, 0)
    other_group = partner_id // seg_count
    other_seg = partner_id % seg_count
    same_group = (other_group[:, None] == other_group[None, :]) & paired[:, None] & paired[None, :]
    send_rank = jnp.sum(same_group & (other_seg[None, :] < other_seg[:, None]), axis=1)
    seg_order = jnp.arange(seg_count)
    recv_rank = jnp.sum(same_group & (seg_order[None, :] < seg_order[:, None]), axis=1)
    target = jnp.where(paired, other_group * slot_most + send_rank, -1)
    source = jnp.where(paired, other_group * slot_most + recv_rank, -1)
    slot_ids = jnp.arange(slots)
    send_hot = (slot_ids[:, None] == target[None, :]).astype(jnp.float32)
    send_hot = send_hot.reshape(slots, face_count, pieces)
    recv_hot = (source[:, None] == slot_ids[None, :]).astype(jnp.float32)
    recv_hot = recv_hot.reshape(face_count, pieces, slots)
    pair_mask = paired.reshape(face_count, 1, pieces, 1, 1)

    x_rows = side6[:, None, :, None] * table_side[None, :, None, :]
    y_rows = table_side[:, None, None, :] * side6[None, :, :, None]
    face_rows = jnp.concatenate(
        [x_rows.reshape(edge * edge, 6 * edge), y_rows.reshape(edge * edge, 6 * edge)], axis=1
    )

    def time_step(_, state):
        small_old, small_cur, plaza_old, plaza_cur = state
        flat_modes = small_cur.reshape(owned, edge * edge, height)
        small_strips = ein("rz,zk->rk", ein("pr,bpk->brk", face_rows, flat_modes).reshape(-1, height), table_height)
        small_strips = small_strips.reshape(owned * 4, 3, edge, height)
        plaza_y = ein("iyk,kz->iyz", ein("ijk,jy->iyk", plaza_cur, side6), table_height)
        plaza_all = gather_slabs(plaza_y.reshape(edge, -1))
        plaza_all = plaza_all.reshape(plaza_len, 6, height)
        plaza_faces = ein("iyz,ix->yxz", plaza_all, plaza_cols)
        plaza_strips = jnp.concatenate(
            [jnp.zeros_like(plaza_faces), plaza_faces], axis=0
        ).reshape(4, 3, edge, height)
        strips = jnp.concatenate([small_strips, plaza_strips], axis=0)
        segments = strips.reshape(face_count, 3, pieces, seg_cells, height)
        outgoing = ein("sfq,fmqcz->smcz", send_hot, segments)
        arrived = lax.all_to_all(outgoing, "rect", 0, 0, tiled=True)
        remote = ein("fqs,smcz->fmqcz", recv_hot, arrived)
        difference = jnp.where(pair_mask, remote - segments, 0.0)
        layers = interface_layers(difference.reshape(face_count, 3, edge, height))
        small_layers = ein("rz,kz->rk", layers[: owned * 4].reshape(-1, height), table_height)
        small_force = ein("pr,brk->bpk", face_rows, small_layers.reshape(owned, -1, height))
        small_force = small_force.reshape(owned, edge, edge, height)
        plaza_layers = ein("fmxz,kz->xfmk", layers[owned * 4 + 2 :], table_height)
        plaza_gathered = gather_slabs(plaza_layers.reshape(edge, -1))
        plaza_gathered = plaza_gathered.reshape(plaza_len, 6, height)
        plaza_x = ein("xyk,ix->iyk", plaza_gathered, plaza_rows)
        plaza_force = ein("iyk,jy->ijk", plaza_x, side6)
        small_next = small_cos * small_cur - small_old + small_gain * small_force
        plaza_next = plaza_cos * plaza_cur - plaza_old + plaza_gain * plaza_force
        return (small_cur, small_next, plaza_cur, plaza_next)

    small_old, small_cur, plaza_old, plaza_cur = lax.fori_loop(
        0, STEPS, time_step, (small_prev, small_now, plaza_prev[0], plaza_now[0])
    )
    return (small_cur, small_old, plaza_cur[None], plaza_old[None])


def solution(mesh):
    return jax.shard_map(
        on_device,
        mesh=mesh,
        in_specs=(
            P(("rect", "split"), None, None, None),
            P(("rect", "split"), None, None, None),
            P("rect", "split", None, None),
            P("rect", "split", None, None),
            P("rect", "split", None),
        ),
        out_specs=(
            P(("rect", "split"), None, None, None),
            P(("rect", "split"), None, None, None),
            P("rect", "split", None, None),
            P("rect", "split", None, None),
        ),
        check_vma=False,
    )
```

```python
import jax
import jax.numpy as jnp
from jax import lax
from jax.sharding import PartitionSpec as P

STEPS = 2
COURANT = 0.5
highest = lax.Precision.HIGHEST


def dct_rows_cols(wavenumber, position, length):
    wavenumber = wavenumber.astype(jnp.float32)[:, None]
    position = position.astype(jnp.float32)[None, :]
    weight = jnp.where(wavenumber == 0.0, jnp.sqrt(1.0 / length), jnp.sqrt(2.0 / length))
    return weight * jnp.cos(jnp.pi * wavenumber * (position + 0.5) / length)


def dct_table(length):
    return dct_rows_cols(jnp.arange(length), jnp.arange(length), length)


def update_factors(first_row, row_count, length_x, edge_cells, height_cells):
    wave_x = (first_row + jnp.arange(row_count)).astype(jnp.float32)[:, None, None] / length_x
    wave_y = jnp.arange(edge_cells, dtype=jnp.float32)[None, :, None] / edge_cells
    wave_z = jnp.arange(height_cells, dtype=jnp.float32)[None, None, :] / height_cells
    phase_angle = COURANT * jnp.pi * jnp.sqrt(wave_x**2 + wave_y**2 + wave_z**2)
    twice_cos = 2.0 * jnp.cos(phase_angle)
    forcing_gain = COURANT**2 * jnp.sinc(phase_angle / (2.0 * jnp.pi)) ** 2
    return (twice_cos, forcing_gain)


def interface_layers(difference):
    nearest = difference[:, 0]
    middle = difference[:, 1]
    farthest = difference[:, 2]
    return jnp.stack(
        [
            (270.0 * nearest - 27.0 * middle + 2.0 * farthest) / 180.0,
            (-27.0 * nearest + 2.0 * middle) / 180.0,
            2.0 * nearest / 180.0,
        ],
        axis=1,
    )


def ein(spec, a, b):
    return jnp.einsum(spec, a, b, precision=highest, preferred_element_type=jnp.float32)


def slab_pieces(block):
    count = lax.axis_size("split")
    pieces = [block]
    for shift in range(1, count):
        perm = [(j, (j - shift) % count) for j in range(count)]
        pieces.append(lax.ppermute(block, "split", perm))
    return pieces


def on_device(small_now, small_prev, plaza_now, plaza_prev, face_partner):
    owned = small_now.shape[0]
    edge = small_now.shape[1]
    height = small_now.shape[3]
    slabs = lax.axis_size("split")
    groups = lax.axis_size("rect")
    plaza_len = edge * slabs
    first_row = lax.axis_index("split") * edge

    table_side = dct_table(edge)
    table_height = dct_table(height)
    edge_pos = jnp.array([0, 1, 2, edge - 1, edge - 2, edge - 3], jnp.int32)
    side6 = table_side[:, edge_pos]
    mine = first_row + jnp.arange(edge)
    slab_of = (lax.axis_index("split") + jnp.arange(slabs)) % slabs
    gathered_rows = (slab_of[:, None] * edge + jnp.arange(edge)[None, :]).reshape(-1)
    plaza_cols = dct_rows_cols(gathered_rows, mine, plaza_len)
    plaza_rows = dct_rows_cols(mine, gathered_rows, plaza_len)
    cols_by_slab = [plaza_cols[t * edge : (t + 1) * edge].T for t in range(slabs)]
    rows_by_slab = [plaza_rows[:, t * edge : (t + 1) * edge] for t in range(slabs)]

    small_cos, small_gain = update_factors(0, edge, edge, edge, height)
    plaza_cos, plaza_gain = update_factors(first_row, edge, plaza_len, edge, height)

    partners = face_partner.reshape(-1)
    seg_count = partners.shape[0]
    face_count = 4 * (owned + 1)
    pieces = seg_count // face_count
    seg_cells = edge // pieces
    unit_count = (2 * owned + 1) * pieces
    slot_most = (unit_count + groups // 2 - 2) // (groups // 2 - 1)
    slots = groups * slot_most
    paired = partners >= 0
    partner_id = jnp.where(paired, partners, 0)
    other_group = partner_id // seg_count
    other_seg = partner_id % seg_count
    same_group = (other_group[:, None] == other_group[None, :]) & paired[:, None] & paired[None, :]
    send_rank = jnp.sum(same_group & (other_seg[None, :] < other_seg[:, None]), axis=1)
    seg_order = jnp.arange(seg_count)
    recv_rank = jnp.sum(same_group & (seg_order[None, :] < seg_order[:, None]), axis=1)
    target = jnp.where(paired, other_group * slot_most + send_rank, -1)
    source = jnp.where(paired, other_group * slot_most + recv_rank, -1)
    slot_ids = jnp.arange(slots)
    send_hot = (slot_ids[:, None] == target[None, :]).astype(jnp.float32)
    send_hot = send_hot.reshape(slots, face_count, pieces)
    recv_hot = (source[:, None] == slot_ids[None, :]).astype(jnp.float32)
    recv_hot = recv_hot.reshape(face_count, pieces, slots)
    pair_mask = paired.reshape(face_count, 1, pieces, 1, 1)

    x_rows = side6[:, None, :, None] * table_side[None, :, None, :]
    y_rows = table_side[:, None, None, :] * side6[None, :, :, None]
    face_rows = jnp.concatenate(
        [x_rows.reshape(edge * edge, 6 * edge), y_rows.reshape(edge * edge, 6 * edge)], axis=1
    )

    def time_step(_, state):
        small_old, small_cur, plaza_old, plaza_cur = state
        flat_modes = small_cur.reshape(owned, edge * edge, height)
        small_strips = ein("rz,zk->rk", ein("pr,bpk->brk", face_rows, flat_modes).reshape(-1, height), table_height)
        small_strips = small_strips.reshape(owned * 4, 3, edge, height)
        plaza_y = ein("iyk,kz->iyz", ein("ijk,jy->iyk", plaza_cur, side6), table_height)
        plaza_faces = sum(
            ein("xi,id->xd", cols_by_slab[t], piece)
            for t, piece in enumerate(slab_pieces(plaza_y.reshape(edge, -1)))
        )
        plaza_faces = jnp.swapaxes(plaza_faces.reshape(edge, 6, height), 0, 1)
        plaza_strips = jnp.concatenate(
            [jnp.zeros_like(plaza_faces), plaza_faces], axis=0
        ).reshape(4, 3, edge, height)
        strips = jnp.concatenate([small_strips, plaza_strips], axis=0)
        segments = strips.reshape(face_count, 3, pieces, seg_cells, height)
        outgoing = ein("sfq,fmqcz->smcz", send_hot, segments)
        arrived = lax.all_to_all(outgoing, "rect", 0, 0, tiled=True)
        remote = ein("fqs,smcz->fmqcz", recv_hot, arrived)
        difference = jnp.where(pair_mask, remote - segments, 0.0)
        layers = interface_layers(difference.reshape(face_count, 3, edge, height))
        small_layers = ein("rz,kz->rk", layers[: owned * 4].reshape(-1, height), table_height)
        small_force = ein("pr,brk->bpk", face_rows, small_layers.reshape(owned, -1, height))
        small_force = small_force.reshape(owned, edge, edge, height)
        plaza_layers = ein("fmxz,kz->xfmk", layers[owned * 4 + 2 :], table_height)
        plaza_x = sum(
            ein("ix,xd->id", rows_by_slab[t], piece)
            for t, piece in enumerate(slab_pieces(plaza_layers.reshape(edge, -1)))
        ).reshape(edge, 6, height)
        plaza_force = ein("iyk,jy->ijk", plaza_x, side6)
        small_next = small_cos * small_cur - small_old + small_gain * small_force
        plaza_next = plaza_cos * plaza_cur - plaza_old + plaza_gain * plaza_force
        return (small_cur, small_next, plaza_cur, plaza_next)

    small_old, small_cur, plaza_old, plaza_cur = lax.fori_loop(
        0, STEPS, time_step, (small_prev, small_now, plaza_prev[0], plaza_now[0])
    )
    return (small_cur, small_old, plaza_cur[None], plaza_old[None])


def solution(mesh):
    return jax.shard_map(
        on_device,
        mesh=mesh,
        in_specs=(
            P(("rect", "split"), None, None, None),
            P(("rect", "split"), None, None, None),
            P("rect", "split", None, None),
            P("rect", "split", None, None),
            P("rect", "split", None),
        ),
        out_specs=(
            P(("rect", "split"), None, None, None),
            P(("rect", "split"), None, None, None),
            P("rect", "split", None, None),
            P("rect", "split", None, None),
        ),
        check_vma=False,
    )
```

```python
import jax
import jax.numpy as jnp
from jax import lax
from jax.sharding import PartitionSpec as P

STEPS = 2
COURANT = 0.5
highest = lax.Precision.HIGHEST


def dct_rows_cols(wavenumber, position, length):
    wavenumber = wavenumber.astype(jnp.float32)[:, None]
    position = position.astype(jnp.float32)[None, :]
    weight = jnp.where(wavenumber == 0.0, jnp.sqrt(1.0 / length), jnp.sqrt(2.0 / length))
    return weight * jnp.cos(jnp.pi * wavenumber * (position + 0.5) / length)


def dct_table(length):
    return dct_rows_cols(jnp.arange(length), jnp.arange(length), length)


def update_factors(first_row, row_count, length_x, edge_cells, height_cells):
    wave_x = (first_row + jnp.arange(row_count)).astype(jnp.float32)[:, None, None] / length_x
    wave_y = jnp.arange(edge_cells, dtype=jnp.float32)[None, :, None] / edge_cells
    wave_z = jnp.arange(height_cells, dtype=jnp.float32)[None, None, :] / height_cells
    phase_angle = COURANT * jnp.pi * jnp.sqrt(wave_x**2 + wave_y**2 + wave_z**2)
    twice_cos = 2.0 * jnp.cos(phase_angle)
    forcing_gain = COURANT**2 * jnp.sinc(phase_angle / (2.0 * jnp.pi)) ** 2
    return (twice_cos, forcing_gain)


def interface_layers(difference):
    nearest = difference[:, 0]
    middle = difference[:, 1]
    farthest = difference[:, 2]
    return jnp.stack(
        [
            (270.0 * nearest - 27.0 * middle + 2.0 * farthest) / 180.0,
            (-27.0 * nearest + 2.0 * middle) / 180.0,
            2.0 * nearest / 180.0,
        ],
        axis=1,
    )


def ein(spec, a, b):
    return jnp.einsum(spec, a, b, precision=highest, preferred_element_type=jnp.float32)


def gather_slabs(block):
    count = lax.axis_size("split")
    pieces = [block]
    for shift in range(1, count):
        perm = [(j, (j - shift) % count) for j in range(count)]
        pieces.append(lax.ppermute(block, "split", perm))
    return jnp.concatenate(pieces, axis=0)


def on_device(small_now, small_prev, plaza_now, plaza_prev, face_partner):
    owned = small_now.shape[0]
    edge = small_now.shape[1]
    height = small_now.shape[3]
    slabs = lax.axis_size("split")
    groups = lax.axis_size("rect")
    plaza_len = edge * slabs
    first_row = lax.axis_index("split") * edge

    table_side = dct_table(edge)
    table_height = dct_table(height)
    edge_pos = jnp.array([0, 1, 2, edge - 1, edge - 2, edge - 3], jnp.int32)
    side6 = table_side[:, edge_pos]
    mine = first_row + jnp.arange(edge)
    slab_of = (lax.axis_index("split") + jnp.arange(slabs)) % slabs
    gathered_rows = (slab_of[:, None] * edge + jnp.arange(edge)[None, :]).reshape(-1)
    plaza_cols = dct_rows_cols(gathered_rows, mine, plaza_len)
    plaza_rows = dct_rows_cols(mine, gathered_rows, plaza_len)

    small_cos, small_gain = update_factors(0, edge, edge, edge, height)
    plaza_cos, plaza_gain = update_factors(first_row, edge, plaza_len, edge, height)

    partners = face_partner.reshape(-1)
    seg_count = partners.shape[0]
    face_count = 4 * (owned + 1)
    pieces = seg_count // face_count
    seg_cells = edge // pieces
    unit_count = (2 * owned + 1) * pieces
    slot_most = (unit_count + groups // 2 - 2) // (groups // 2 - 1)
    slots = groups * slot_most
    paired = partners >= 0
    partner_id = jnp.where(paired, partners, 0)
    other_group = partner_id // seg_count
    other_seg = partner_id % seg_count
    same_group = (other_group[:, None] == other_group[None, :]) & paired[:, None] & paired[None, :]
    send_rank = jnp.sum(same_group & (other_seg[None, :] < other_seg[:, None]), axis=1)
    seg_order = jnp.arange(seg_count)
    recv_rank = jnp.sum(same_group & (seg_order[None, :] < seg_order[:, None]), axis=1)
    target = jnp.where(paired, other_group * slot_most + send_rank, -1)
    source = jnp.where(paired, other_group * slot_most + recv_rank, -1)
    slot_ids = jnp.arange(slots)
    send_hot = (slot_ids[:, None] == target[None, :]).astype(jnp.float32)
    send_hot = send_hot.reshape(slots, face_count, pieces)
    recv_hot = (source[:, None] == slot_ids[None, :]).astype(jnp.float32)
    recv_hot = recv_hot.reshape(face_count, pieces, slots)
    pair_mask = paired.reshape(face_count, 1, pieces, 1, 1)

    x_rows = side6[:, None, :, None] * table_side[None, :, None, :]
    y_rows = table_side[:, None, None, :] * side6[None, :, :, None]
    face_rows = jnp.concatenate(
        [x_rows.reshape(edge * edge, 6 * edge), y_rows.reshape(edge * edge, 6 * edge)], axis=1
    )

    def time_step(_, state):
        small_cur, small_step, plaza_cur, plaza_step = state
        small_old = small_cur - small_step
        plaza_old = plaza_cur - plaza_step
        flat_modes = small_cur.reshape(owned, edge * edge, height)
        small_strips = ein("rz,zk->rk", ein("pr,bpk->brk", face_rows, flat_modes).reshape(-1, height), table_height)
        small_strips = small_strips.reshape(owned * 4, 3, edge, height)
        plaza_y = ein("iyk,kz->iyz", ein("ijk,jy->iyk", plaza_cur, side6), table_height)
        plaza_all = gather_slabs(plaza_y.reshape(edge, -1))
        plaza_all = plaza_all.reshape(plaza_len, 6, height)
        plaza_faces = ein("iyz,ix->yxz", plaza_all, plaza_cols)
        plaza_strips = jnp.concatenate(
            [jnp.zeros_like(plaza_faces), plaza_faces], axis=0
        ).reshape(4, 3, edge, height)
        strips = jnp.concatenate([small_strips, plaza_strips], axis=0)
        segments = strips.reshape(face_count, 3, pieces, seg_cells, height)
        outgoing = ein("sfq,fmqcz->smcz", send_hot, segments)
        arrived = lax.all_to_all(outgoing, "rect", 0, 0, tiled=True)
        remote = ein("fqs,smcz->fmqcz", recv_hot, arrived)
        difference = jnp.where(pair_mask, remote - segments, 0.0)
        layers = interface_layers(difference.reshape(face_count, 3, edge, height))
        small_layers = ein("rz,kz->rk", layers[: owned * 4].reshape(-1, height), table_height)
        small_force = ein("pr,brk->bpk", face_rows, small_layers.reshape(owned, -1, height))
        small_force = small_force.reshape(owned, edge, edge, height)
        plaza_layers = ein("fmxz,kz->xfmk", layers[owned * 4 + 2 :], table_height)
        plaza_gathered = gather_slabs(plaza_layers.reshape(edge, -1))
        plaza_gathered = plaza_gathered.reshape(plaza_len, 6, height)
        plaza_x = ein("xyk,ix->iyk", plaza_gathered, plaza_rows)
        plaza_force = ein("iyk,jy->ijk", plaza_x, side6)
        small_next = small_cos * small_cur - small_old + small_gain * small_force
        plaza_next = plaza_cos * plaza_cur - plaza_old + plaza_gain * plaza_force
        return (small_next, small_next - small_cur, plaza_next, plaza_next - plaza_cur)

    start = (small_now, small_now - small_prev, plaza_now[0], plaza_now[0] - plaza_prev[0])
    small_cur, small_step, plaza_cur, plaza_step = lax.fori_loop(0, STEPS, time_step, start)
    small_old = small_cur - small_step
    plaza_old = plaza_cur - plaza_step
    return (small_cur, small_old, plaza_cur[None], plaza_old[None])


def solution(mesh):
    return jax.shard_map(
        on_device,
        mesh=mesh,
        in_specs=(
            P(("rect", "split"), None, None, None),
            P(("rect", "split"), None, None, None),
            P("rect", "split", None, None),
            P("rect", "split", None, None),
            P("rect", "split", None),
        ),
        out_specs=(
            P(("rect", "split"), None, None, None),
            P(("rect", "split"), None, None, None),
            P("rect", "split", None, None),
            P("rect", "split", None, None),
        ),
        check_vma=False,
    )
```

```python
import jax
import jax.numpy as jnp
from jax import lax
from jax.sharding import PartitionSpec as P

STEPS = 2
COURANT = 0.5
highest = lax.Precision.HIGHEST


def dct_rows_cols(wavenumber, position, length):
    wavenumber = wavenumber.astype(jnp.float32)[:, None]
    position = position.astype(jnp.float32)[None, :]
    weight = jnp.where(wavenumber == 0.0, jnp.sqrt(1.0 / length), jnp.sqrt(2.0 / length))
    return weight * jnp.cos(jnp.pi * wavenumber * (position + 0.5) / length)


def dct_table(length):
    return dct_rows_cols(jnp.arange(length), jnp.arange(length), length)


def update_factors(first_row, row_count, length_x, edge_cells, height_cells):
    wave_x = (first_row + jnp.arange(row_count)).astype(jnp.float32)[:, None, None] / length_x
    wave_y = jnp.arange(edge_cells, dtype=jnp.float32)[None, :, None] / edge_cells
    wave_z = jnp.arange(height_cells, dtype=jnp.float32)[None, None, :] / height_cells
    phase_angle = COURANT * jnp.pi * jnp.sqrt(wave_x**2 + wave_y**2 + wave_z**2)
    twice_cos = 2.0 * jnp.cos(phase_angle)
    forcing_gain = COURANT**2 * jnp.sinc(phase_angle / (2.0 * jnp.pi)) ** 2
    return (twice_cos, forcing_gain)


def interface_layers(difference):
    nearest = difference[:, 0]
    middle = difference[:, 1]
    farthest = difference[:, 2]
    return jnp.stack(
        [
            (270.0 * nearest - 27.0 * middle + 2.0 * farthest) / 180.0,
            (-27.0 * nearest + 2.0 * middle) / 180.0,
            2.0 * nearest / 180.0,
        ],
        axis=1,
    )


def ein(spec, a, b):
    return jnp.einsum(spec, a, b, precision=highest, preferred_element_type=jnp.float32)


def gather_slabs(block):
    count = lax.axis_size("split")
    pieces = [block]
    for shift in range(1, count):
        perm = [(j, (j - shift) % count) for j in range(count)]
        pieces.append(lax.ppermute(block, "split", perm))
    return jnp.concatenate(pieces, axis=0)


def on_device(small_now, small_prev, plaza_now, plaza_prev, face_partner):
    owned = small_now.shape[0]
    edge = small_now.shape[1]
    height = small_now.shape[3]
    slabs = lax.axis_size("split")
    groups = lax.axis_size("rect")
    plaza_len = edge * slabs
    first_row = lax.axis_index("split") * edge

    table_side = dct_table(edge)
    table_height = dct_table(height)
    edge_pos = jnp.array([0, 1, 2, edge - 1, edge - 2, edge - 3], jnp.int32)
    side6 = table_side[:, edge_pos]
    mine = first_row + jnp.arange(edge)
    slab_of = (lax.axis_index("split") + jnp.arange(slabs)) % slabs
    gathered_rows = (slab_of[:, None] * edge + jnp.arange(edge)[None, :]).reshape(-1)
    plaza_cols = dct_rows_cols(gathered_rows, mine, plaza_len)
    plaza_rows = dct_rows_cols(mine, gathered_rows, plaza_len)
    plaza_cols_t = plaza_cols.T

    small_cos, small_gain = update_factors(0, edge, edge, edge, height)
    plaza_cos, plaza_gain = update_factors(first_row, edge, plaza_len, edge, height)

    partners = face_partner.reshape(-1)
    seg_count = partners.shape[0]
    face_count = 4 * (owned + 1)
    pieces = seg_count // face_count
    seg_cells = edge // pieces
    unit_count = (2 * owned + 1) * pieces
    slot_most = (unit_count + groups // 2 - 2) // (groups // 2 - 1)
    slots = groups * slot_most
    paired = partners >= 0
    partner_id = jnp.where(paired, partners, 0)
    other_group = partner_id // seg_count
    other_seg = partner_id % seg_count
    same_group = (other_group[:, None] == other_group[None, :]) & paired[:, None] & paired[None, :]
    send_rank = jnp.sum(same_group & (other_seg[None, :] < other_seg[:, None]), axis=1)
    seg_order = jnp.arange(seg_count)
    recv_rank = jnp.sum(same_group & (seg_order[None, :] < seg_order[:, None]), axis=1)
    target = jnp.where(paired, other_group * slot_most + send_rank, -1)
    source = jnp.where(paired, other_group * slot_most + recv_rank, -1)
    slot_ids = jnp.arange(slots)
    send_hot = (slot_ids[:, None] == target[None, :]).astype(jnp.float32)
    send_hot = send_hot.reshape(slots, face_count, pieces)
    recv_hot = (source[:, None] == slot_ids[None, :]).astype(jnp.float32)
    recv_hot = recv_hot.reshape(face_count, pieces, slots)
    pair_mask = paired.reshape(face_count, 1, pieces, 1, 1)

    x_rows = side6[:, None, :, None] * table_side[None, :, None, :]
    y_rows = table_side[:, None, None, :] * side6[None, :, :, None]
    face_rows = jnp.concatenate(
        [x_rows.reshape(edge * edge, 6 * edge), y_rows.reshape(edge * edge, 6 * edge)], axis=1
    )

    small_old, small_cur = small_prev, small_now
    plaza_old, plaza_cur = plaza_prev[0], plaza_now[0]
    for _ in range(STEPS):
        flat_modes = small_cur.reshape(owned, edge * edge, height)
        small_strips = ein("rz,zk->rk", ein("pr,bpk->brk", face_rows, flat_modes).reshape(-1, height), table_height)
        small_strips = small_strips.reshape(owned * 4, 3, edge, height)
        plaza_y = ein("iyk,kz->iyz", ein("ijk,jy->iyk", plaza_cur, side6), table_height)
        plaza_all = gather_slabs(plaza_y.reshape(edge, -1))
        plaza_faces = ein("xi,id->xd", plaza_cols_t, plaza_all)
        plaza_faces = jnp.swapaxes(plaza_faces.reshape(edge, 6, height), 0, 1)
        plaza_strips = jnp.concatenate(
            [jnp.zeros_like(plaza_faces), plaza_faces], axis=0
        ).reshape(4, 3, edge, height)
        strips = jnp.concatenate([small_strips, plaza_strips], axis=0)
        segments = strips.reshape(face_count, 3, pieces, seg_cells, height)
        outgoing = ein("sfq,fmqcz->smcz", send_hot, segments)
        arrived = lax.all_to_all(outgoing, "rect", 0, 0, tiled=True)
        remote = ein("fqs,smcz->fmqcz", recv_hot, arrived)
        difference = jnp.where(pair_mask, remote - segments, 0.0)
        layers = interface_layers(difference.reshape(face_count, 3, edge, height))
        small_layers = ein("rz,kz->rk", layers[: owned * 4].reshape(-1, height), table_height)
        small_force = ein("pr,brk->bpk", face_rows, small_layers.reshape(owned, -1, height))
        small_force = small_force.reshape(owned, edge, edge, height)
        plaza_layers = ein("fmxz,kz->xfmk", layers[owned * 4 + 2 :], table_height)
        plaza_gathered = gather_slabs(plaza_layers.reshape(edge, -1))
        plaza_x = ein("ix,xd->id", plaza_rows, plaza_gathered).reshape(edge, 6, height)
        plaza_force = ein("iyk,jy->ijk", plaza_x, side6)
        small_next = small_cos * small_cur - small_old + small_gain * small_force
        plaza_next = plaza_cos * plaza_cur - plaza_old + plaza_gain * plaza_force
        small_old, small_cur = small_cur, small_next
        plaza_old, plaza_cur = plaza_cur, plaza_next
    return (small_cur, small_old, plaza_cur[None], plaza_old[None])


def solution(mesh):
    return jax.shard_map(
        on_device,
        mesh=mesh,
        in_specs=(
            P(("rect", "split"), None, None, None),
            P(("rect", "split"), None, None, None),
            P("rect", "split", None, None),
            P("rect", "split", None, None),
            P("rect", "split", None),
        ),
        out_specs=(
            P(("rect", "split"), None, None, None),
            P(("rect", "split"), None, None, None),
            P("rect", "split", None, None),
            P("rect", "split", None, None),
        ),
        check_vma=False,
    )
```

```python
import jax
import jax.numpy as jnp
from jax import lax
from jax.sharding import PartitionSpec as P

STEPS = 2
COURANT = 0.5
highest = lax.Precision.HIGHEST


def dct_rows_cols(wavenumber, position, length):
    wavenumber = wavenumber.astype(jnp.float32)[:, None]
    position = position.astype(jnp.float32)[None, :]
    weight = jnp.where(wavenumber == 0.0, jnp.sqrt(1.0 / length), jnp.sqrt(2.0 / length))
    return weight * jnp.cos(jnp.pi * wavenumber * (position + 0.5) / length)


def dct_table(length):
    return dct_rows_cols(jnp.arange(length), jnp.arange(length), length)


def update_factors(first_row, row_count, length_x, edge_cells, height_cells):
    wave_x = (first_row + jnp.arange(row_count)).astype(jnp.float32)[:, None, None] / length_x
    wave_y = jnp.arange(edge_cells, dtype=jnp.float32)[None, :, None] / edge_cells
    wave_z = jnp.arange(height_cells, dtype=jnp.float32)[None, None, :] / height_cells
    phase_angle = COURANT * jnp.pi * jnp.sqrt(wave_x**2 + wave_y**2 + wave_z**2)
    twice_cos = 2.0 * jnp.cos(phase_angle)
    forcing_gain = COURANT**2 * jnp.sinc(phase_angle / (2.0 * jnp.pi)) ** 2
    return (twice_cos, forcing_gain)


def interface_layers(difference):
    nearest = difference[:, 0]
    middle = difference[:, 1]
    farthest = difference[:, 2]
    return jnp.stack(
        [
            (270.0 * nearest - 27.0 * middle + 2.0 * farthest) / 180.0,
            (-27.0 * nearest + 2.0 * middle) / 180.0,
            2.0 * nearest / 180.0,
        ],
        axis=1,
    )


def ein(spec, a, b):
    return jnp.einsum(spec, a, b, precision=highest, preferred_element_type=jnp.float32)


def gather_slabs(block):
    count = lax.axis_size("split")
    pieces = [block]
    for shift in range(1, count):
        perm = [(j, (j - shift) % count) for j in range(count)]
        pieces.append(lax.ppermute(block, "split", perm))
    return jnp.concatenate(pieces, axis=0)


def on_device(small_now, small_prev, plaza_now, plaza_prev, face_partner):
    owned = small_now.shape[0]
    edge = small_now.shape[1]
    height = small_now.shape[3]
    slabs = lax.axis_size("split")
    groups = lax.axis_size("rect")
    plaza_len = edge * slabs
    first_row = lax.axis_index("split") * edge

    table_side = dct_table(edge)
    table_height = dct_table(height)
    edge_pos = jnp.array([0, 1, 2, edge - 1, edge - 2, edge - 3], jnp.int32)
    side6 = table_side[:, edge_pos]
    mine = first_row + jnp.arange(edge)
    slab_of = (lax.axis_index("split") + jnp.arange(slabs)) % slabs
    gathered_rows = (slab_of[:, None] * edge + jnp.arange(edge)[None, :]).reshape(-1)
    plaza_cols = dct_rows_cols(gathered_rows, mine, plaza_len)
    plaza_rows = dct_rows_cols(mine, gathered_rows, plaza_len)
    plaza_cols_t = plaza_cols.T

    small_cos, small_gain = update_factors(0, edge, edge, edge, height)
    plaza_cos, plaza_gain = update_factors(first_row, edge, plaza_len, edge, height)

    partners = face_partner.reshape(-1)
    seg_count = partners.shape[0]
    face_count = 4 * (owned + 1)
    pieces = seg_count // face_count
    seg_cells = edge // pieces
    unit_count = (2 * owned + 1) * pieces
    slot_most = (unit_count + groups // 2 - 2) // (groups // 2 - 1)
    slots = groups * slot_most
    paired = partners >= 0
    partner_id = jnp.where(paired, partners, 0)
    other_group = partner_id // seg_count
    other_seg = partner_id % seg_count
    same_group = (other_group[:, None] == other_group[None, :]) & paired[:, None] & paired[None, :]
    send_rank = jnp.sum(same_group & (other_seg[None, :] < other_seg[:, None]), axis=1)
    seg_order = jnp.arange(seg_count)
    recv_rank = jnp.sum(same_group & (seg_order[None, :] < seg_order[:, None]), axis=1)
    target = jnp.where(paired, other_group * slot_most + send_rank, -1)
    source = jnp.where(paired, other_group * slot_most + recv_rank, -1)
    slot_ids = jnp.arange(slots)
    send_hot = (slot_ids[:, None] == target[None, :]).astype(jnp.float32)
    send_hot = send_hot.reshape(slots, face_count, pieces)
    recv_hot = (source[:, None] == slot_ids[None, :]).astype(jnp.float32)
    recv_hot = recv_hot.reshape(face_count, pieces, slots)
    pair_mask = paired.reshape(face_count, 1, pieces, 1, 1)
    slot_used = jnp.any(slot_ids[:, None] == target[None, :], axis=1)
    slot_source = jnp.where(slot_used, jnp.argmax(slot_ids[:, None] == target[None, :], axis=1), seg_count)
    seg_source = jnp.where(paired, source, slots)

    x_rows = side6[:, None, :, None] * table_side[None, :, None, :]
    y_rows = table_side[:, None, None, :] * side6[None, :, :, None]
    face_rows = jnp.concatenate(
        [x_rows.reshape(edge * edge, 6 * edge), y_rows.reshape(edge * edge, 6 * edge)], axis=1
    )

    small_old, small_cur = small_prev, small_now
    plaza_old, plaza_cur = plaza_prev[0], plaza_now[0]
    for _ in range(STEPS):
        flat_modes = small_cur.reshape(owned, edge * edge, height)
        small_strips = ein("rz,zk->rk", ein("pr,bpk->brk", face_rows, flat_modes).reshape(-1, height), table_height)
        small_strips = small_strips.reshape(owned * 4, 3, edge, height)
        plaza_y = ein("iyk,kz->iyz", ein("ijk,jy->iyk", plaza_cur, side6), table_height)
        plaza_all = gather_slabs(plaza_y.reshape(edge, -1))
        plaza_faces = ein("xi,id->xd", plaza_cols_t, plaza_all)
        plaza_faces = jnp.swapaxes(plaza_faces.reshape(edge, 6, height), 0, 1)
        plaza_strips = jnp.concatenate(
            [jnp.zeros_like(plaza_faces), plaza_faces], axis=0
        ).reshape(4, 3, edge, height)
        strips = jnp.concatenate([small_strips, plaza_strips], axis=0)
        segments = strips.reshape(face_count, 3, pieces, seg_cells, height)
        by_segment = jnp.transpose(segments, (0, 2, 1, 3, 4)).reshape(seg_count, 3, seg_cells, height)
        outgoing = jnp.take(by_segment, slot_source, axis=0, mode="fill", fill_value=0.0)
        arrived = lax.all_to_all(outgoing, "rect", 0, 0, tiled=True)
        remote = jnp.take(arrived, seg_source, axis=0, mode="fill", fill_value=0.0)
        remote = jnp.transpose(remote.reshape(face_count, pieces, 3, seg_cells, height), (0, 2, 1, 3, 4))
        difference = jnp.where(pair_mask, remote - segments, 0.0)
        layers = interface_layers(difference.reshape(face_count, 3, edge, height))
        small_layers = ein("rz,kz->rk", layers[: owned * 4].reshape(-1, height), table_height)
        small_force = ein("pr,brk->bpk", face_rows, small_layers.reshape(owned, -1, height))
        small_force = small_force.reshape(owned, edge, edge, height)
        plaza_layers = ein("fmxz,kz->xfmk", layers[owned * 4 + 2 :], table_height)
        plaza_gathered = gather_slabs(plaza_layers.reshape(edge, -1))
        plaza_x = ein("ix,xd->id", plaza_rows, plaza_gathered).reshape(edge, 6, height)
        plaza_force = ein("iyk,jy->ijk", plaza_x, side6)
        small_next = small_cos * small_cur - small_old + small_gain * small_force
        plaza_next = plaza_cos * plaza_cur - plaza_old + plaza_gain * plaza_force
        small_old, small_cur = small_cur, small_next
        plaza_old, plaza_cur = plaza_cur, plaza_next
    return (small_cur, small_old, plaza_cur[None], plaza_old[None])


def solution(mesh):
    return jax.shard_map(
        on_device,
        mesh=mesh,
        in_specs=(
            P(("rect", "split"), None, None, None),
            P(("rect", "split"), None, None, None),
            P("rect", "split", None, None),
            P("rect", "split", None, None),
            P("rect", "split", None),
        ),
        out_specs=(
            P(("rect", "split"), None, None, None),
            P(("rect", "split"), None, None, None),
            P("rect", "split", None, None),
            P("rect", "split", None, None),
        ),
        check_vma=False,
    )
```

```python
import jax
import jax.numpy as jnp
from jax import lax
from jax.sharding import PartitionSpec as P

STEPS = 2
COURANT = 0.5
highest = lax.Precision.HIGHEST


def dct_rows_cols(wavenumber, position, length):
    wavenumber = wavenumber.astype(jnp.float32)[:, None]
    position = position.astype(jnp.float32)[None, :]
    weight = jnp.where(wavenumber == 0.0, jnp.sqrt(1.0 / length), jnp.sqrt(2.0 / length))
    return weight * jnp.cos(jnp.pi * wavenumber * (position + 0.5) / length)


def dct_table(length):
    return dct_rows_cols(jnp.arange(length), jnp.arange(length), length)


def update_factors(first_row, row_count, length_x, edge_cells, height_cells):
    wave_x = (first_row + jnp.arange(row_count)).astype(jnp.float32)[:, None, None] / length_x
    wave_y = jnp.arange(edge_cells, dtype=jnp.float32)[None, :, None] / edge_cells
    wave_z = jnp.arange(height_cells, dtype=jnp.float32)[None, None, :] / height_cells
    phase_angle = COURANT * jnp.pi * jnp.sqrt(wave_x**2 + wave_y**2 + wave_z**2)
    twice_cos = 2.0 * jnp.cos(phase_angle)
    forcing_gain = COURANT**2 * jnp.sinc(phase_angle / (2.0 * jnp.pi)) ** 2
    return (twice_cos, forcing_gain)


def interface_layers(difference):
    nearest = difference[:, 0]
    middle = difference[:, 1]
    farthest = difference[:, 2]
    return jnp.stack(
        [
            (270.0 * nearest - 27.0 * middle + 2.0 * farthest) / 180.0,
            (-27.0 * nearest + 2.0 * middle) / 180.0,
            2.0 * nearest / 180.0,
        ],
        axis=1,
    )


def ein(spec, a, b):
    return jnp.einsum(spec, a, b, precision=highest, preferred_element_type=jnp.float32)


def gather_slabs(block):
    count = lax.axis_size("split")
    pieces = [block]
    for shift in range(1, count):
        perm = [(j, (j - shift) % count) for j in range(count)]
        pieces.append(lax.ppermute(block, "split", perm))
    return jnp.concatenate(pieces, axis=0)


def on_device(small_now, small_prev, plaza_now, plaza_prev, face_partner):
    owned = small_now.shape[0]
    edge = small_now.shape[1]
    height = small_now.shape[3]
    slabs = lax.axis_size("split")
    groups = lax.axis_size("rect")
    plaza_len = edge * slabs
    first_row = lax.axis_index("split") * edge

    table_side = dct_table(edge)
    table_height = dct_table(height)
    edge_pos = jnp.array([0, 1, 2, edge - 1, edge - 2, edge - 3], jnp.int32)
    side6 = table_side[:, edge_pos]
    mine = first_row + jnp.arange(edge)
    slab_of = (lax.axis_index("split") + jnp.arange(slabs)) % slabs
    gathered_rows = (slab_of[:, None] * edge + jnp.arange(edge)[None, :]).reshape(-1)
    plaza_cols = dct_rows_cols(gathered_rows, mine, plaza_len)
    plaza_rows = dct_rows_cols(mine, gathered_rows, plaza_len)
    plaza_cols_t = plaza_cols.T
    plaza_project = jnp.eye(edge, dtype=jnp.float32)[:, None, :, None] * side6.T[None, :, None, :]
    plaza_project = plaza_project.reshape(edge * 6, edge * edge)

    small_cos, small_gain = update_factors(0, edge, edge, edge, height)
    plaza_cos, plaza_gain = update_factors(first_row, edge, plaza_len, edge, height)

    partners = face_partner.reshape(-1)
    seg_count = partners.shape[0]
    face_count = 4 * (owned + 1)
    pieces = seg_count // face_count
    seg_cells = edge // pieces
    unit_count = (2 * owned + 1) * pieces
    slot_most = (unit_count + groups // 2 - 2) // (groups // 2 - 1)
    slots = groups * slot_most
    paired = partners >= 0
    partner_id = jnp.where(paired, partners, 0)
    other_group = partner_id // seg_count
    other_seg = partner_id % seg_count
    same_group = (other_group[:, None] == other_group[None, :]) & paired[:, None] & paired[None, :]
    send_rank = jnp.sum(same_group & (other_seg[None, :] < other_seg[:, None]), axis=1)
    seg_order = jnp.arange(seg_count)
    recv_rank = jnp.sum(same_group & (seg_order[None, :] < seg_order[:, None]), axis=1)
    target = jnp.where(paired, other_group * slot_most + send_rank, -1)
    source = jnp.where(paired, other_group * slot_most + recv_rank, -1)
    slot_ids = jnp.arange(slots)
    send_hot = (slot_ids[:, None] == target[None, :]).astype(jnp.float32)
    send_hot = send_hot.reshape(slots, face_count, pieces)
    recv_hot = (source[:, None] == slot_ids[None, :]).astype(jnp.float32)
    recv_hot = recv_hot.reshape(face_count, pieces, slots)
    pair_mask = paired.reshape(face_count, 1, pieces, 1, 1)

    x_rows = side6[:, None, :, None] * table_side[None, :, None, :]
    y_rows = table_side[:, None, None, :] * side6[None, :, :, None]
    face_rows = jnp.concatenate(
        [x_rows.reshape(edge * edge, 6 * edge), y_rows.reshape(edge * edge, 6 * edge)], axis=1
    )

    small_old, small_cur = small_prev, small_now
    plaza_old, plaza_cur = plaza_prev[0], plaza_now[0]
    for _ in range(STEPS):
        flat_modes = small_cur.reshape(owned, edge * edge, height)
        small_strips = ein("rz,zk->rk", ein("pr,bpk->brk", face_rows, flat_modes).reshape(-1, height), table_height)
        small_strips = small_strips.reshape(owned * 4, 3, edge, height)
        plaza_y = ein("rk,kz->rz", ein("rp,pk->rk", plaza_project, plaza_cur.reshape(-1, height)), table_height)
        plaza_all = gather_slabs(plaza_y.reshape(edge, -1))
        plaza_faces = ein("xi,id->xd", plaza_cols_t, plaza_all)
        plaza_faces = jnp.swapaxes(plaza_faces.reshape(edge, 6, height), 0, 1)
        plaza_strips = jnp.concatenate(
            [jnp.zeros_like(plaza_faces), plaza_faces], axis=0
        ).reshape(4, 3, edge, height)
        strips = jnp.concatenate([small_strips, plaza_strips], axis=0)
        segments = strips.reshape(face_count, 3, pieces, seg_cells, height)
        outgoing = ein("sfq,fmqcz->smcz", send_hot, segments)
        arrived = lax.all_to_all(outgoing, "rect", 0, 0, tiled=True)
        remote = ein("fqs,smcz->fmqcz", recv_hot, arrived)
        difference = jnp.where(pair_mask, remote - segments, 0.0)
        layers = interface_layers(difference.reshape(face_count, 3, edge, height))
        small_layers = ein("rz,kz->rk", layers[: owned * 4].reshape(-1, height), table_height)
        small_force = ein("pr,brk->bpk", face_rows, small_layers.reshape(owned, -1, height))
        small_force = small_force.reshape(owned, edge, edge, height)
        plaza_layers = ein("fmxz,kz->xfmk", layers[owned * 4 + 2 :], table_height)
        plaza_gathered = gather_slabs(plaza_layers.reshape(edge, -1))
        plaza_x = ein("ix,xd->id", plaza_rows, plaza_gathered).reshape(edge, 6, height)
        plaza_force = ein("pr,rk->pk", plaza_project.T, plaza_x.reshape(-1, height)).reshape(edge, edge, height)
        small_next = small_cos * small_cur - small_old + small_gain * small_force
        plaza_next = plaza_cos * plaza_cur - plaza_old + plaza_gain * plaza_force
        small_old, small_cur = small_cur, small_next
        plaza_old, plaza_cur = plaza_cur, plaza_next
    return (small_cur, small_old, plaza_cur[None], plaza_old[None])


def solution(mesh):
    return jax.shard_map(
        on_device,
        mesh=mesh,
        in_specs=(
            P(("rect", "split"), None, None, None),
            P(("rect", "split"), None, None, None),
            P("rect", "split", None, None),
            P("rect", "split", None, None),
            P("rect", "split", None),
        ),
        out_specs=(
            P(("rect", "split"), None, None, None),
            P(("rect", "split"), None, None, None),
            P("rect", "split", None, None),
            P("rect", "split", None, None),
        ),
        check_vma=False,
    )
```

```python
import jax
import jax.numpy as jnp
from jax import lax
from jax.sharding import PartitionSpec as P

STEPS = 2
COURANT = 0.5
highest = lax.Precision.HIGHEST


def dct_rows_cols(wavenumber, position, length):
    wavenumber = wavenumber.astype(jnp.float32)[:, None]
    position = position.astype(jnp.float32)[None, :]
    weight = jnp.where(wavenumber == 0.0, jnp.sqrt(1.0 / length), jnp.sqrt(2.0 / length))
    return weight * jnp.cos(jnp.pi * wavenumber * (position + 0.5) / length)


def dct_table(length):
    return dct_rows_cols(jnp.arange(length), jnp.arange(length), length)


def update_factors(first_row, row_count, length_x, edge_cells, height_cells):
    wave_x = (first_row + jnp.arange(row_count)).astype(jnp.float32)[:, None, None] / length_x
    wave_y = jnp.arange(edge_cells, dtype=jnp.float32)[None, :, None] / edge_cells
    wave_z = jnp.arange(height_cells, dtype=jnp.float32)[None, None, :] / height_cells
    phase_angle = COURANT * jnp.pi * jnp.sqrt(wave_x**2 + wave_y**2 + wave_z**2)
    twice_cos = 2.0 * jnp.cos(phase_angle)
    forcing_gain = COURANT**2 * jnp.sinc(phase_angle / (2.0 * jnp.pi)) ** 2
    return (twice_cos, forcing_gain)


def interface_layers(difference):
    nearest = difference[:, 0]
    middle = difference[:, 1]
    farthest = difference[:, 2]
    return jnp.stack(
        [
            (270.0 * nearest - 27.0 * middle + 2.0 * farthest) / 180.0,
            (-27.0 * nearest + 2.0 * middle) / 180.0,
            2.0 * nearest / 180.0,
        ],
        axis=1,
    )


def ein(spec, a, b):
    return jnp.einsum(spec, a, b, precision=highest, preferred_element_type=jnp.float32)


def gather_slabs(block):
    count = lax.axis_size("split")
    pieces = [block]
    for shift in range(1, count):
        perm = [(j, (j - shift) % count) for j in range(count)]
        pieces.append(lax.ppermute(block, "split", perm))
    return jnp.concatenate(pieces, axis=0)


def on_device(small_now, small_prev, plaza_now, plaza_prev, face_partner):
    owned = small_now.shape[0]
    edge = small_now.shape[1]
    height = small_now.shape[3]
    slabs = lax.axis_size("split")
    groups = lax.axis_size("rect")
    plaza_len = edge * slabs
    first_row = lax.axis_index("split") * edge

    table_side = dct_table(edge)
    table_height = dct_table(height)
    edge_pos = jnp.array([0, 1, 2, edge - 1, edge - 2, edge - 3], jnp.int32)
    side6 = table_side[:, edge_pos]
    mine = first_row + jnp.arange(edge)
    slab_of = (lax.axis_index("split") + jnp.arange(slabs)) % slabs
    gathered_rows = (slab_of[:, None] * edge + jnp.arange(edge)[None, :]).reshape(-1)
    plaza_cols = dct_rows_cols(gathered_rows, mine, plaza_len)
    plaza_rows = dct_rows_cols(mine, gathered_rows, plaza_len)
    plaza_cols_t = plaza_cols.T

    small_cos, small_gain = update_factors(0, edge, edge, edge, height)
    plaza_cos, plaza_gain = update_factors(first_row, edge, plaza_len, edge, height)
    response = jnp.einsum(
        "jw,ijk,jy->iwyk", side6, plaza_gain, side6, precision=highest,
        preferred_element_type=jnp.float32,
    )

    partners = face_partner.reshape(-1)
    seg_count = partners.shape[0]
    face_count = 4 * (owned + 1)
    pieces = seg_count // face_count
    seg_cells = edge // pieces
    unit_count = (2 * owned + 1) * pieces
    slot_most = (unit_count + groups // 2 - 2) // (groups // 2 - 1)
    slots = groups * slot_most
    paired = partners >= 0
    partner_id = jnp.where(paired, partners, 0)
    other_group = partner_id // seg_count
    other_seg = partner_id % seg_count
    same_group = (other_group[:, None] == other_group[None, :]) & paired[:, None] & paired[None, :]
    send_rank = jnp.sum(same_group & (other_seg[None, :] < other_seg[:, None]), axis=1)
    seg_order = jnp.arange(seg_count)
    recv_rank = jnp.sum(same_group & (seg_order[None, :] < seg_order[:, None]), axis=1)
    target = jnp.where(paired, other_group * slot_most + send_rank, -1)
    source = jnp.where(paired, other_group * slot_most + recv_rank, -1)
    slot_ids = jnp.arange(slots)
    send_hot = (slot_ids[:, None] == target[None, :]).astype(jnp.float32)
    send_hot = send_hot.reshape(slots, face_count, pieces)
    recv_hot = (source[:, None] == slot_ids[None, :]).astype(jnp.float32)
    recv_hot = recv_hot.reshape(face_count, pieces, slots)
    pair_mask = paired.reshape(face_count, 1, pieces, 1, 1)

    x_rows = side6[:, None, :, None] * table_side[None, :, None, :]
    y_rows = table_side[:, None, None, :] * side6[None, :, :, None]
    face_rows = jnp.concatenate(
        [x_rows.reshape(edge * edge, 6 * edge), y_rows.reshape(edge * edge, 6 * edge)], axis=1
    )

    small_old, small_cur = small_prev, small_now
    plaza_old, plaza_cur = plaza_prev[0], plaza_now[0]
    for step in range(STEPS):
        flat_modes = small_cur.reshape(owned, edge * edge, height)
        small_strips = ein("rz,zk->rk", ein("pr,bpk->brk", face_rows, flat_modes).reshape(-1, height), table_height)
        small_strips = small_strips.reshape(owned * 4, 3, edge, height)
        if step == 0:
            plaza_pre = ein("ijk,jy->iyk", plaza_cur, side6)
        plaza_y = ein("iyk,kz->iyz", plaza_pre, table_height)
        plaza_all = gather_slabs(plaza_y.reshape(edge, -1))
        plaza_faces = ein("xi,id->xd", plaza_cols_t, plaza_all)
        plaza_faces = jnp.swapaxes(plaza_faces.reshape(edge, 6, height), 0, 1)
        plaza_strips = jnp.concatenate(
            [jnp.zeros_like(plaza_faces), plaza_faces], axis=0
        ).reshape(4, 3, edge, height)
        strips = jnp.concatenate([small_strips, plaza_strips], axis=0)
        segments = strips.reshape(face_count, 3, pieces, seg_cells, height)
        outgoing = ein("sfq,fmqcz->smcz", send_hot, segments)
        arrived = lax.all_to_all(outgoing, "rect", 0, 0, tiled=True)
        remote = ein("fqs,smcz->fmqcz", recv_hot, arrived)
        difference = jnp.where(pair_mask, remote - segments, 0.0)
        layers = interface_layers(difference.reshape(face_count, 3, edge, height))
        small_layers = ein("rz,kz->rk", layers[: owned * 4].reshape(-1, height), table_height)
        small_force = ein("pr,brk->bpk", face_rows, small_layers.reshape(owned, -1, height))
        small_force = small_force.reshape(owned, edge, edge, height)
        plaza_layers = ein("fmxz,kz->xfmk", layers[owned * 4 + 2 :], table_height)
        plaza_gathered = gather_slabs(plaza_layers.reshape(edge, -1))
        plaza_x = ein("ix,xd->id", plaza_rows, plaza_gathered).reshape(edge, 6, height)
        plaza_force = ein("iyk,jy->ijk", plaza_x, side6)
        if step < STEPS - 1:
            plaza_pre = ein("ijk,jy->iyk", plaza_cos * plaza_cur - plaza_old, side6) + jnp.sum(
                response * plaza_x[:, None, :, :], axis=2
            )
        small_next = small_cos * small_cur - small_old + small_gain * small_force
        plaza_next = plaza_cos * plaza_cur - plaza_old + plaza_gain * plaza_force
        small_old, small_cur = small_cur, small_next
        plaza_old, plaza_cur = plaza_cur, plaza_next
    return (small_cur, small_old, plaza_cur[None], plaza_old[None])


def solution(mesh):
    return jax.shard_map(
        on_device,
        mesh=mesh,
        in_specs=(
            P(("rect", "split"), None, None, None),
            P(("rect", "split"), None, None, None),
            P("rect", "split", None, None),
            P("rect", "split", None, None),
            P("rect", "split", None),
        ),
        out_specs=(
            P(("rect", "split"), None, None, None),
            P(("rect", "split"), None, None, None),
            P("rect", "split", None, None),
            P("rect", "split", None, None),
        ),
        check_vma=False,
    )
```

```python
import jax
import jax.numpy as jnp
from jax import lax
from jax.sharding import PartitionSpec as P

STEPS = 2
COURANT = 0.5
highest = lax.Precision.HIGHEST


def dct_rows_cols(wavenumber, position, length):
    wavenumber = wavenumber.astype(jnp.float32)[:, None]
    position = position.astype(jnp.float32)[None, :]
    weight = jnp.where(wavenumber == 0.0, jnp.sqrt(1.0 / length), jnp.sqrt(2.0 / length))
    return weight * jnp.cos(jnp.pi * wavenumber * (position + 0.5) / length)


def dct_table(length):
    return dct_rows_cols(jnp.arange(length), jnp.arange(length), length)


def update_factors(first_row, row_count, length_x, edge_cells, height_cells):
    wave_x = (first_row + jnp.arange(row_count)).astype(jnp.float32)[:, None, None] / length_x
    wave_y = jnp.arange(edge_cells, dtype=jnp.float32)[None, :, None] / edge_cells
    wave_z = jnp.arange(height_cells, dtype=jnp.float32)[None, None, :] / height_cells
    phase_angle = COURANT * jnp.pi * jnp.sqrt(wave_x**2 + wave_y**2 + wave_z**2)
    twice_cos = 2.0 * jnp.cos(phase_angle)
    forcing_gain = COURANT**2 * jnp.sinc(phase_angle / (2.0 * jnp.pi)) ** 2
    return (twice_cos, forcing_gain)


def interface_layers(difference):
    nearest = difference[:, 0]
    middle = difference[:, 1]
    farthest = difference[:, 2]
    return jnp.stack(
        [
            (270.0 * nearest - 27.0 * middle + 2.0 * farthest) / 180.0,
            (-27.0 * nearest + 2.0 * middle) / 180.0,
            2.0 * nearest / 180.0,
        ],
        axis=1,
    )


def ein(spec, a, b):
    return jnp.einsum(spec, a, b, precision=highest, preferred_element_type=jnp.float32)


def gather_slabs(block):
    count = lax.axis_size("split")
    pieces = [block]
    for shift in range(1, count):
        perm = [(j, (j - shift) % count) for j in range(count)]
        pieces.append(lax.ppermute(block, "split", perm))
    return jnp.concatenate(pieces, axis=0)


def on_device(small_now, small_prev, plaza_now, plaza_prev, face_partner):
    owned = small_now.shape[0]
    edge = small_now.shape[1]
    height = small_now.shape[3]
    slabs = lax.axis_size("split")
    groups = lax.axis_size("rect")
    plaza_len = edge * slabs
    first_row = lax.axis_index("split") * edge

    table_side = dct_table(edge)
    table_height = dct_table(height)
    edge_pos = jnp.array([0, 1, 2, edge - 1, edge - 2, edge - 3], jnp.int32)
    side6 = table_side[:, edge_pos]
    mine = first_row + jnp.arange(edge)
    slab_of = (lax.axis_index("split") + jnp.arange(slabs)) % slabs
    gathered_rows = (slab_of[:, None] * edge + jnp.arange(edge)[None, :]).reshape(-1)
    plaza_cols = dct_rows_cols(gathered_rows, mine, plaza_len)
    plaza_rows = dct_rows_cols(mine, gathered_rows, plaza_len)
    plaza_cols_t = plaza_cols.T

    small_cos, small_gain = update_factors(0, edge, edge, edge, height)
    plaza_cos, plaza_gain = update_factors(first_row, edge, plaza_len, edge, height)

    partners = face_partner.reshape(-1)
    seg_count = partners.shape[0]
    face_count = 4 * (owned + 1)
    pieces = seg_count // face_count
    seg_cells = edge // pieces
    unit_count = (2 * owned + 1) * pieces
    slot_most = (unit_count + groups // 2 - 2) // (groups // 2 - 1)
    slots = groups * slot_most
    paired = partners >= 0
    partner_id = jnp.where(paired, partners, 0)
    other_group = partner_id // seg_count
    other_seg = partner_id % seg_count
    same_group = (other_group[:, None] == other_group[None, :]) & paired[:, None] & paired[None, :]
    send_rank = jnp.sum(same_group & (other_seg[None, :] < other_seg[:, None]), axis=1)
    seg_order = jnp.arange(seg_count)
    recv_rank = jnp.sum(same_group & (seg_order[None, :] < seg_order[:, None]), axis=1)
    target = jnp.where(paired, other_group * slot_most + send_rank, -1)
    source = jnp.where(paired, other_group * slot_most + recv_rank, -1)
    slot_ids = jnp.arange(slots)
    send_hot = (slot_ids[:, None] == target[None, :]).astype(jnp.float32)
    send_hot = send_hot.reshape(slots, face_count, pieces)
    recv_hot = (source[:, None] == slot_ids[None, :]).astype(jnp.float32)
    recv_hot = recv_hot.reshape(face_count, pieces, slots)
    pair_mask = paired.reshape(face_count, 1, pieces, 1, 1)

    x_rows = side6[:, None, :, None] * table_side[None, :, None, :]
    y_rows = table_side[:, None, None, :] * side6[None, :, :, None]
    face_rows = jnp.concatenate(
        [x_rows.reshape(edge * edge, 6 * edge), y_rows.reshape(edge * edge, 6 * edge)], axis=1
    )

    def time_step(_, state):
        small_old, small_cur, plaza_old, plaza_cur = state
        flat_modes = small_cur.reshape(owned, edge * edge, height)
        small_strips = ein("rz,zk->rk", ein("pr,bpk->brk", face_rows, flat_modes).reshape(-1, height), table_height)
        small_strips = small_strips.reshape(owned * 4, 3, edge, height)
        plaza_y = ein("iyk,kz->iyz", ein("ijk,jy->iyk", plaza_cur, side6), table_height)
        plaza_all = gather_slabs(plaza_y.reshape(edge, -1))
        plaza_faces = ein("xi,id->xd", plaza_cols_t, plaza_all)
        plaza_faces = jnp.swapaxes(plaza_faces.reshape(edge, 6, height), 0, 1)
        plaza_strips = jnp.concatenate(
            [jnp.zeros_like(plaza_faces), plaza_faces], axis=0
        ).reshape(4, 3, edge, height)
        strips = jnp.concatenate([small_strips, plaza_strips], axis=0)
        segments = strips.reshape(face_count, 3, pieces, seg_cells, height)
        outgoing = ein("sfq,fmqcz->smcz", send_hot, segments)
        arrived = lax.all_to_all(outgoing, "rect", 0, 0, tiled=True)
        remote = ein("fqs,smcz->fmqcz", recv_hot, arrived)
        difference = jnp.where(pair_mask, remote - segments, 0.0)
        layers = interface_layers(difference.reshape(face_count, 3, edge, height))
        small_layers = ein("rz,kz->rk", layers[: owned * 4].reshape(-1, height), table_height)
        small_force = ein("pr,brk->bpk", face_rows, small_layers.reshape(owned, -1, height))
        small_force = small_force.reshape(owned, edge, edge, height)
        plaza_layers = ein("fmxz,kz->xfmk", layers[owned * 4 + 2 :], table_height)
        plaza_gathered = gather_slabs(plaza_layers.reshape(edge, -1))
        plaza_x = ein("ix,xd->id", plaza_rows, plaza_gathered).reshape(edge, 6, height)
        plaza_force = ein("iyk,jy->ijk", plaza_x, side6)
        small_next = small_cos * small_cur - small_old + small_gain * small_force
        plaza_next = plaza_cos * plaza_cur - plaza_old + plaza_gain * plaza_force
        return (small_cur, small_next, plaza_cur, plaza_next)

    small_old, small_cur, plaza_old, plaza_cur = lax.fori_loop(
        0, STEPS, time_step, (small_prev, small_now, plaza_prev[0], plaza_now[0])
    )
    return (small_cur, small_old, plaza_cur[None], plaza_old[None])


def solution(mesh):
    return jax.shard_map(
        on_device,
        mesh=mesh,
        in_specs=(
            P(("rect", "split"), None, None, None),
            P(("rect", "split"), None, None, None),
            P("rect", "split", None, None),
            P("rect", "split", None, None),
            P("rect", "split", None),
        ),
        out_specs=(
            P(("rect", "split"), None, None, None),
            P(("rect", "split"), None, None, None),
            P("rect", "split", None, None),
            P("rect", "split", None, None),
        ),
        check_vma=False,
    )
```
